512 devices in a mesh: grp: 2 (over core), dp: 32 (over x_hi, z), seq: 8 (over y, x_lo).
Axes of the slice: x: 4 (x_hi: 2, x_lo: 2; x = x_hi * 2 + x_lo), y: 4, z: 16, core: 2. Of those that a mesh axis runs over, the one named last changes fastest.
Arguments:
- latents: float32 [64, 256, 2432], P(('grp', 'dp'), None, 'seq'), may hold values from -6 to 6
- step_noise: bfloat16 [2, 64, 256, 2432], P(None, ('grp', 'dp'), None, 'seq'), may hold values from -6 to 6
- ada_table: float32 [10, 2, 2432], replicated
- qkv_weight: bfloat16 [3, 2048, 2432], P(None, 'seq', ('grp', 'dp')), may hold values from -0.125 to 0.125
- out_weight: bfloat16 [2048, 2432], P(('grp', 'dp'), 'seq'), may hold values from -0.125 to 0.125
- rewards: float32 [64], replicated, may hold values from -4 to 4
- group_ids: int32 [64], replicated, may hold values from 0 to 7, as said below
- time_index: int32 [64], P(('grp', 'dp')), may hold values from 1 to 8
- log_ratio: float32 [2, 64], replicated, may hold values from -0.4 to 0.4
Outputs:
- final_latents: float32 [64, 256, 2432], P(('grp', 'dp'), None, 'seq')
- policy_loss: float32 [], replicated
- out_grad: float32 [2048, 2432], P(('grp', 'dp'), 'seq')
The draws below stay inside these ranges and needn't reach their ends.
Inputs may be any that keep to these rules, and one draw needn't show every extreme that they name: `group_ids`: each group number names exactly 8 samples.
All inputs are finite; a program needn't handle non-finite values.
Results may differ from the reference program's by a relative error of at most 0.017.
Values may be sent and summed in bfloat16 or wider, within the bound.
No kernel may reach another device: no remote copies, remote signals or barrier semaphores. Data moves between devices by JAX's collectives and lax.ppermute only.
A program may use at most 64 MiB of HBM per device.

```python
import jax
import jax.numpy as jnp
from jax import lax

D = 2432
HEADS = 32
HD = 64
L = 256
TSTEPS = 10
GSIZE = 8
SAMPLES = 64


def draw_ada_table(key, part):
    first, second = jax.random.split(jax.random.fold_in(key, 11))
    scale = 0.3 * jax.random.normal(first, (TSTEPS, D), jnp.float32)
    shift = 0.3 * jax.random.normal(second, (TSTEPS, D), jnp.float32)
    return jnp.stack([scale, shift], 1).astype(jnp.float32)


def draw_group_ids(key, part):
    order = jax.random.permutation(jax.random.fold_in(key, 23), SAMPLES)
    return (order // GSIZE).astype(jnp.int32)


def with_ends(values, key, low, high):
    index_at = [jax.random.randint(jax.random.fold_in(key, axis), (), 0, length) for axis, length in enumerate(values.shape)]
    longest = values.shape.index(max(values.shape))
    next_to = index_at[:longest] + [(index_at[longest] + 1) % values.shape[longest]] + index_at[longest + 1:]
    return values.at[tuple(index_at)].set(low).at[tuple(next_to)].set(high)


def shard_levels(own_key, dims, shards, low, largest):
    gain, own = 1.0, jax.random.fold_in(own_key, 6)
    for dim, shards_of in shards:
        steps = jnp.exp(jax.random.uniform(jax.random.fold_in(own, dim), (shards_of,), jnp.float32, low / len(shards), largest / len(shards)))
        gain = gain * jnp.repeat(steps, dims[dim] // shards_of).reshape([-1 if axis == dim else 1 for axis in range(len(dims))])
    return gain


def scatter_about(key, extent, scale, reach, pieces=(), dtype=jnp.bfloat16):
    loudness = shard_levels(key, extent, pieces, -0.22, 0.18) if pieces else 1.0
    array = jax.random.normal(key, extent, jnp.float32) * scale * loudness
    return jnp.minimum(jnp.maximum(array, -reach), reach).astype(dtype)


def setup_inputs(seed: int = 0) -> dict:
    keys = jax.random.split(jax.random.key(seed), 10)
    return {
        "latents": scatter_about(keys[0], (SAMPLES, L, D), 1.0, 6.0, ((0, 64), (2, 8)), jnp.float32),
        "step_noise": scatter_about(keys[1], (2, SAMPLES, L, D), 1.0, 6.0, ((1, 64), (3, 8))),
        "ada_table": draw_ada_table(jax.random.fold_in(keys[9], 71), 0),
        "qkv_weight": scatter_about(keys[3], (3, HEADS * HD, D), D ** -0.5, 0.125, ((1, 8), (2, 64))),
        "out_weight": scatter_about(keys[4], (HEADS * HD, D), (HEADS * HD) ** -0.5, 0.125, ((0, 64), (1, 8))),
        "rewards": scatter_about(keys[5], (SAMPLES,), 1.0, 4.0, (), jnp.float32),
        "group_ids": draw_group_ids(jax.random.fold_in(keys[9], 71), 0),
        "time_index": with_ends(jax.random.randint(keys[7], (SAMPLES,), 1, TSTEPS - 1), jax.random.fold_in(keys[7], 1), 1, (TSTEPS - 1) - 1).astype(jnp.int32),
        "log_ratio": jnp.clip(jax.random.uniform(keys[8], (2, SAMPLES), jnp.float32, -0.4, 0.4), -0.4, 0.4),
    }


SDE_NOISE = 0.7
CLIP_RANGE = 0.2
REWARD_FLOOR = 0.75
NORM_EPS = 1e-06

def advantages(rewards, group_ids):
    same_group = (group_ids[:, None] == group_ids[None, :]).astype(jnp.float32)
    centre = lax.optimization_barrier(jnp.sum(same_group * rewards[None, :], 1)) / GSIZE
    spread = lax.optimization_barrier(jnp.sum(same_group * (rewards[None, :] - centre[:, None]) ** 2, 1)) / GSIZE
    return (rewards - centre) / jnp.maximum(jnp.sqrt(spread), REWARD_FLOOR)

def policy_terms(advantage, log_ratio):
    ratios = jnp.exp(log_ratio)
    plain = ratios * advantage[None, :]
    bounded = jnp.clip(ratios, 1.0 - CLIP_RANGE, 1.0 + CLIP_RANGE) * advantage[None, :]
    count = 2.0 * advantage.shape[0]
    loss_value = -jnp.sum(jnp.minimum(plain, bounded)) / count
    coef = jnp.where(plain <= bounded, -plain / count, jnp.float32(0.0))
    return (loss_value, coef)

def reference(latents, step_noise, ada_table, qkv_weight, out_weight, rewards, group_ids, time_index, log_ratio):
    advantage = advantages(rewards, group_ids)
    loss_value, coef = policy_terms(advantage, log_ratio)
    step_size = 1.0 / TSTEPS
    projection = qkv_weight.reshape(3 * HEADS * HD, D)

    def forward_one(inputs):
        state, modulate = inputs
        centre = lax.optimization_barrier(jnp.mean(state, -1, keepdims=True))
        spread = lax.optimization_barrier(jnp.mean((state - centre) ** 2, -1, keepdims=True))
        normed = ((state - centre) * lax.rsqrt(spread + NORM_EPS) * (1.0 + modulate[0][None, :]) + modulate[1][None, :]).astype(jnp.bfloat16)
        proj = lax.dot_general(normed, projection, (((1,), (1,)), ((), ())), preferred_element_type=jnp.float32).astype(jnp.bfloat16)
        proj = proj.reshape(L, 3, HEADS, HD).astype(jnp.float32)
        logits = jnp.einsum('qhe,khe->hqk', proj[:, 0], proj[:, 1]) * HD ** (-0.5)
        logits = logits - lax.optimization_barrier(jnp.max(logits, -1, keepdims=True))
        weights = jnp.exp(logits)
        probs = (weights / lax.optimization_barrier(jnp.sum(weights, -1, keepdims=True))).astype(jnp.bfloat16)
        attn = jnp.einsum('hqk,khe->qhe', probs.astype(jnp.float32), proj[:, 2]).astype(jnp.bfloat16)
        attn = attn.reshape(L, HEADS * HD)
        velocity = jnp.dot(attn, out_weight, preferred_element_type=jnp.float32)
        return (attn, velocity)
    state = latents
    gradient = jnp.zeros((HEADS * HD, D), jnp.float32)
    for section in range(2):
        index_now = (time_index + section).astype(jnp.int32)
        time_now = 1.0 - index_now.astype(jnp.float32) / TSTEPS
        modulate = ada_table[index_now]
        attn, velocity = lax.map(forward_one, (state, modulate))
        noise_level = SDE_NOISE * SDE_NOISE * time_now / (1.0 - time_now)
        std_dev = jnp.sqrt(noise_level * step_size)
        level = noise_level[:, None, None]
        time_col = time_now[:, None, None]
        drift = velocity + level / (2.0 * time_col) * (state + (1.0 - time_col) * velocity)
        centre = state - step_size * drift
        noise_now = step_noise[section].astype(jnp.float32)
        state = centre + std_dev[:, None, None] * noise_now
        factor = coef[section] * -step_size * (1.0 + noise_level * (1.0 - time_now) / (2.0 * time_now)) / std_dev
        score = (factor[:, None, None] * noise_now).astype(jnp.bfloat16)
        gradient = gradient + jnp.einsum('blh,bld->hd', attn.astype(jnp.float32), score.astype(jnp.float32))
    return (state, loss_value, gradient)
```

```python
import jax
import jax.numpy as jnp
from jax import lax
from jax.sharding import Mesh
from jax.sharding import PartitionSpec as P

HD = 64
TSTEPS = 10
GSIZE = 8


SDE_NOISE = 0.7
CLIP_RANGE = 0.2
REWARD_FLOOR = 0.75
NORM_EPS = 1e-06

SAMPLE_AXES = ("grp", "xh", "z")
FEATURE_AXES = ("y", "xl")


def advantages(rewards, group_ids):
    same_group = (group_ids[:, None] == group_ids[None, :]).astype(jnp.float32)
    centre = jnp.sum(same_group * rewards[None, :], 1) / GSIZE
    spread = jnp.sum(same_group * (rewards[None, :] - centre[:, None]) ** 2, 1) / GSIZE
    return (rewards - centre) / jnp.maximum(jnp.sqrt(spread), REWARD_FLOOR)


def policy_terms(advantage, log_ratio):
    ratios = jnp.exp(log_ratio)
    plain = ratios * advantage[None, :]
    bounded = jnp.clip(ratios, 1.0 - CLIP_RANGE, 1.0 + CLIP_RANGE) * advantage[None, :]
    count = 2.0 * advantage.shape[0]
    loss_value = -jnp.sum(jnp.minimum(plain, bounded)) / count
    coef = jnp.where(plain <= bounded, -plain / count, jnp.float32(0.0))
    return (loss_value, coef)


def gather_all_to_all(x, axis_name, size):
    spread = jnp.broadcast_to(x[None], (size,) + x.shape)
    return lax.all_to_all(spread, axis_name, 0, 0, tiled=True)


def gather_pair(x, axis_name):
    other = lax.ppermute(x, axis_name, [(0, 1), (1, 0)])
    first = lax.axis_index(axis_name) == 0
    return jnp.where(first, jnp.stack([x, other]), jnp.stack([other, x]))


def reduce_pair(x, axis_name):
    me = lax.axis_index(axis_name)
    keep = lax.dynamic_index_in_dim(x, me, 0, keepdims=False)
    send = lax.dynamic_index_in_dim(x, 1 - me, 0, keepdims=False)
    return keep + lax.ppermute(send, axis_name, [(0, 1), (1, 0)])


def on_device(
    latents,
    step_noise,
    ada_table,
    qkv_weight,
    out_weight,
    rewards,
    group_ids,
    time_index,
    log_ratio,
    z_size,
    seq_size,
):
    qkv_shape = qkv_weight.shape
    out_shape = out_weight.shape
    packed = jnp.concatenate([qkv_weight.reshape(-1), out_weight.reshape(-1)])
    packed = gather_all_to_all(packed, "z", z_size)
    packed = gather_pair(packed, "xh")
    packed = gather_pair(packed, "grp")
    owners = packed.shape[0] * packed.shape[1] * packed.shape[2]
    packed = packed.reshape(owners, -1)
    qkv_size = qkv_shape[0] * qkv_shape[1] * qkv_shape[2]
    qkv_parts = packed[:, :qkv_size].reshape(owners, qkv_shape[0], qkv_shape[1], qkv_shape[2])
    qkv_full = jnp.transpose(qkv_parts, (1, 2, 0, 3)).reshape(
        qkv_shape[0], qkv_shape[1], owners * qkv_shape[2]
    )
    out_rows = packed[:, qkv_size:].reshape(owners * out_shape[0], out_shape[1])

    group_width = qkv_full.shape[1]
    heads_here = group_width // HD
    model_width = qkv_full.shape[2]
    projection = qkv_full.reshape(3 * group_width, model_width)
    samples = rewards.shape[0]
    seq_len = latents.shape[1]
    block_rows = min(512, seq_len)
    advantage = advantages(rewards, group_ids)
    loss_value, coef = policy_terms(advantage, log_ratio)
    my_index = lax.axis_index(SAMPLE_AXES)
    chooser = (jnp.arange(samples, dtype=jnp.int32) == my_index).astype(jnp.float32)
    my_coef = jnp.sum(coef * chooser[None, :], 1)
    step_size = 1.0 / TSTEPS
    state = latents[0]
    attn_list = []
    score_list = []
    plan = jnp.arange(TSTEPS, dtype=jnp.int32)
    for section in range(2):
        index_now = time_index[0] + section
        time_now = 1.0 - index_now.astype(jnp.float32) / TSTEPS
        picker = (plan == index_now).astype(jnp.float32)
        modulate = jnp.sum(picker[:, None, None] * ada_table, 0)
        blocks = gather_all_to_all(state, FEATURE_AXES, seq_size)
        whole = jnp.transpose(blocks, (1, 0, 2)).reshape(seq_len, -1)
        centre = jnp.mean(whole, -1, keepdims=True)
        spread = jnp.mean((whole - centre) ** 2, -1, keepdims=True)
        normed = (
            (whole - centre) * lax.rsqrt(spread + NORM_EPS) * (1.0 + modulate[0][None, :])
            + modulate[1][None, :]
        ).astype(jnp.bfloat16)
        proj_rows = lax.dot_general(
            normed, projection, (((1,), (1,)), ((), ())), preferred_element_type=jnp.float32
        ).astype(jnp.bfloat16)
        proj_rows = proj_rows.reshape(seq_len, 3, heads_here, HD)
        key_rows = proj_rows[:, 1]
        value_rows = proj_rows[:, 2]
        query_rows = proj_rows[0:block_rows, 0]
        logits = jnp.einsum(
            "qhe,khe->hqk", query_rows, key_rows, preferred_element_type=jnp.float32
        ) * HD ** (-0.5)
        logits = logits - jnp.max(logits, -1, keepdims=True)
        weights = jnp.exp(logits)
        probs = (weights / jnp.sum(weights, -1, keepdims=True)).astype(jnp.bfloat16)
        attn_blocks = jnp.einsum(
            "hqk,khe->qhe", probs, value_rows, preferred_element_type=jnp.float32
        ).astype(jnp.bfloat16)
        attn = attn_blocks.reshape(seq_len, group_width)
        attn_parts = gather_all_to_all(attn, FEATURE_AXES, seq_size)
        attn_all = jnp.transpose(attn_parts, (1, 0, 2)).reshape(seq_len, -1)
        velocity = jnp.dot(attn_all, out_rows, preferred_element_type=jnp.float32)
        noise_level = SDE_NOISE * SDE_NOISE * time_now / (1.0 - time_now)
        std_dev = jnp.sqrt(noise_level * step_size)
        drift = velocity + noise_level / (2.0 * time_now) * (state + (1.0 - time_now) * velocity)
        mean_next = state - step_size * drift
        noise_now = step_noise[section, 0].astype(jnp.float32)
        state = mean_next + std_dev * noise_now
        factor = (
            my_coef[section]
            * -step_size
            * (1.0 + noise_level * (1.0 - time_now) / (2.0 * time_now))
            / std_dev
        )
        score_list.append((factor * noise_now).astype(jnp.bfloat16))
        attn_list.append(attn_all)
    attn_both = jnp.stack(attn_list, 0)
    score_both = jnp.stack(score_list, 0)
    gradient = lax.dot_general(
        attn_both, score_both, (((0, 1), (0, 1)), ((), ())), preferred_element_type=jnp.float32
    )
    rows = gradient.shape[0]
    part = gradient.reshape(2, rows // 2, -1)
    part = reduce_pair(part, "grp")
    part = part.reshape(2, rows // 4, -1)
    part = reduce_pair(part, "xh")
    part = part.reshape(z_size, rows // (4 * z_size), -1)
    part = lax.all_to_all(part, "z", 0, 0, tiled=True)
    out_grad = jnp.sum(part, 0)
    return (state[None], loss_value, out_grad)


def solution(mesh):
    grp, dp, seq = (mesh.shape[a] for a in ("grp", "dp", "seq"))
    xh, xl = 2, 2
    z_size, y_size = dp // xh, seq // xl
    fine = Mesh(
        mesh.devices.reshape(grp, xh, z_size, y_size, xl), ("grp", "xh", "z", "y", "xl")
    )
    samples = SAMPLE_AXES
    features = FEATURE_AXES

    def body(*args):
        return on_device(*args, z_size=z_size, seq_size=seq)

    return jax.shard_map(
        body,
        mesh=fine,
        in_specs=(
            P(samples, None, features),
            P(None, samples, None, features),
            P(),
            P(None, features, samples),
            P(samples, features),
            P(),
            P(),
            P(samples),
            P(),
        ),
        out_specs=(P(samples, None, features), P(), P(samples, features)),
        check_vma=False,
    )
```

```python
import jax
import jax.numpy as jnp
from jax import lax
from jax.sharding import Mesh
from jax.sharding import PartitionSpec as P

HD = 64
TSTEPS = 10
GSIZE = 8


SDE_NOISE = 0.7
CLIP_RANGE = 0.2
REWARD_FLOOR = 0.75
NORM_EPS = 1e-06

SAMPLE_AXES = ("grp", "xh", "z")
FEATURE_AXES = ("y", "xl")


def advantages(rewards, group_ids):
    same_group = (group_ids[:, None] == group_ids[None, :]).astype(jnp.float32)
    centre = jnp.sum(same_group * rewards[None, :], 1) / GSIZE
    spread = jnp.sum(same_group * (rewards[None, :] - centre[:, None]) ** 2, 1) / GSIZE
    return (rewards - centre) / jnp.maximum(jnp.sqrt(spread), REWARD_FLOOR)


def policy_terms(advantage, log_ratio):
    ratios = jnp.exp(log_ratio)
    plain = ratios * advantage[None, :]
    bounded = jnp.clip(ratios, 1.0 - CLIP_RANGE, 1.0 + CLIP_RANGE) * advantage[None, :]
    count = 2.0 * advantage.shape[0]
    loss_value = -jnp.sum(jnp.minimum(plain, bounded)) / count
    coef = jnp.where(plain <= bounded, -plain / count, jnp.float32(0.0))
    return (loss_value, coef)


def gather_all_to_all(x, axis_name, size):
    spread = jnp.broadcast_to(x[None], (size,) + x.shape)
    return lax.all_to_all(spread, axis_name, 0, 0, tiled=True)


def gather_pair(x, axis_name):
    other = lax.ppermute(x, axis_name, [(0, 1), (1, 0)])
    first = lax.axis_index(axis_name) == 0
    return jnp.where(first, jnp.stack([x, other]), jnp.stack([other, x]))


def reduce_pair(x, axis_name):
    me = lax.axis_index(axis_name)
    keep = lax.dynamic_index_in_dim(x, me, 0, keepdims=False)
    send = lax.dynamic_index_in_dim(x, 1 - me, 0, keepdims=False)
    sent = lax.ppermute(send.astype(jnp.bfloat16), axis_name, [(0, 1), (1, 0)])
    return keep + sent.astype(keep.dtype)


def on_device(
    latents,
    step_noise,
    ada_table,
    qkv_weight,
    out_weight,
    rewards,
    group_ids,
    time_index,
    log_ratio,
    z_size,
    seq_size,
):
    units = qkv_weight.shape[0] * qkv_weight.shape[1]
    qkv_t = jnp.transpose(qkv_weight, (2, 0, 1)).reshape(qkv_weight.shape[2], units)
    qkv_t = lax.all_gather(qkv_t, "z", axis=0, tiled=True)
    qkv_t = gather_pair(qkv_t, "xh").reshape(-1, units)
    projection_t = gather_pair(qkv_t, "grp").reshape(-1, units)
    out_rows = lax.all_gather(out_weight, "z", axis=0, tiled=True)
    out_rows = gather_pair(out_rows, "xh").reshape(-1, out_weight.shape[1])
    out_rows = gather_pair(out_rows, "grp").reshape(-1, out_weight.shape[1])

    group_width = qkv_weight.shape[1]
    heads_here = group_width // HD
    samples = rewards.shape[0]
    seq_len = latents.shape[1]
    block_rows = min(512, seq_len)
    advantage = advantages(rewards, group_ids)
    loss_value, coef = policy_terms(advantage, log_ratio)
    my_index = lax.axis_index(SAMPLE_AXES)
    chooser = (jnp.arange(samples, dtype=jnp.int32) == my_index).astype(jnp.float32)
    my_coef = jnp.sum(coef * chooser[None, :], 1)
    step_size = 1.0 / TSTEPS
    state = latents[0]
    attn_list = []
    score_list = []
    plan = jnp.arange(TSTEPS, dtype=jnp.int32)
    for section in range(2):
        index_now = time_index[0] + section
        time_now = 1.0 - index_now.astype(jnp.float32) / TSTEPS
        picker = (plan == index_now).astype(jnp.float32)
        modulate = jnp.sum(picker[:, None, None] * ada_table, 0)
        blocks = gather_all_to_all(state, FEATURE_AXES, seq_size)
        whole = jnp.transpose(blocks, (1, 0, 2)).reshape(seq_len, -1)
        centre = jnp.mean(whole, -1, keepdims=True)
        spread = jnp.mean((whole - centre) ** 2, -1, keepdims=True)
        normed = (
            (whole - centre) * lax.rsqrt(spread + NORM_EPS) * (1.0 + modulate[0][None, :])
            + modulate[1][None, :]
        ).astype(jnp.bfloat16)
        proj_rows = jnp.dot(normed, projection_t, preferred_element_type=jnp.float32).astype(
            jnp.bfloat16
        )
        proj_rows = proj_rows.reshape(seq_len, 3, heads_here, HD)
        key_rows = proj_rows[:, 1]
        value_rows = proj_rows[:, 2]
        query_rows = proj_rows[0:block_rows, 0]
        logits = jnp.einsum(
            "qhe,khe->hqk", query_rows, key_rows, preferred_element_type=jnp.float32
        ) * HD ** (-0.5)
        logits = logits - jnp.max(logits, -1, keepdims=True)
        weights = jnp.exp(logits)
        probs = (weights / jnp.sum(weights, -1, keepdims=True)).astype(jnp.bfloat16)
        attn_blocks = jnp.einsum(
            "hqk,khe->qhe", probs, value_rows, preferred_element_type=jnp.float32
        ).astype(jnp.bfloat16)
        attn = attn_blocks.reshape(seq_len, group_width)
        attn_parts = gather_all_to_all(attn, FEATURE_AXES, seq_size)
        attn_all = jnp.transpose(attn_parts, (1, 0, 2)).reshape(seq_len, -1)
        velocity = jnp.dot(attn_all, out_rows, preferred_element_type=jnp.float32)
        noise_level = SDE_NOISE * SDE_NOISE * time_now / (1.0 - time_now)
        std_dev = jnp.sqrt(noise_level * step_size)
        drift = velocity + noise_level / (2.0 * time_now) * (state + (1.0 - time_now) * velocity)
        mean_next = state - step_size * drift
        noise_now = step_noise[section, 0].astype(jnp.float32)
        state = mean_next + std_dev * noise_now
        factor = (
            my_coef[section]
            * -step_size
            * (1.0 + noise_level * (1.0 - time_now) / (2.0 * time_now))
            / std_dev
        )
        score_list.append((factor * noise_now).astype(jnp.bfloat16))
        attn_list.append(attn_all)
    attn_both = jnp.stack(attn_list, 0)
    score_both = jnp.stack(score_list, 0)
    gradient = lax.dot_general(
        attn_both, score_both, (((0, 1), (0, 1)), ((), ())), preferred_element_type=jnp.float32
    )
    rows = gradient.shape[0]
    part = gradient.reshape(2, rows // 2, -1)
    part = reduce_pair(part, "grp")
    part = part.reshape(2, rows // 4, -1)
    part = reduce_pair(part, "xh")
    part = part.reshape(z_size, rows // (4 * z_size), -1)
    part = lax.all_to_all(part.astype(jnp.bfloat16), "z", 0, 0, tiled=True)
    out_grad = jnp.sum(part.astype(jnp.float32), 0)
    return (state[None], loss_value, out_grad)


def solution(mesh):
    grp, dp, seq = (mesh.shape[a] for a in ("grp", "dp", "seq"))
    xh, xl = 2, 2
    z_size, y_size = dp // xh, seq // xl
    fine = Mesh(
        mesh.devices.reshape(grp, xh, z_size, y_size, xl), ("grp", "xh", "z", "y", "xl")
    )
    samples = SAMPLE_AXES
    features = FEATURE_AXES

    def body(*args):
        return on_device(*args, z_size=z_size, seq_size=seq)

    return jax.shard_map(
        body,
        mesh=fine,
        in_specs=(
            P(samples, None, features),
            P(None, samples, None, features),
            P(),
            P(None, features, samples),
            P(samples, features),
            P(),
            P(),
            P(samples),
            P(),
        ),
        out_specs=(P(samples, None, features), P(), P(samples, features)),
        check_vma=False,
    )
```

```python
import jax
import jax.numpy as jnp
from jax import lax
from jax.sharding import Mesh
from jax.sharding import PartitionSpec as P

HD = 64
TSTEPS = 10
GSIZE = 8


SDE_NOISE = 0.7
CLIP_RANGE = 0.2
REWARD_FLOOR = 0.75
NORM_EPS = 1e-06

SAMPLE_AXES = ("grp", "xh", "z")
FEATURE_AXES = ("y", "xl")


def advantages(rewards, group_ids):
    same_group = (group_ids[:, None] == group_ids[None, :]).astype(jnp.float32)
    centre = jnp.sum(same_group * rewards[None, :], 1) / GSIZE
    spread = jnp.sum(same_group * (rewards[None, :] - centre[:, None]) ** 2, 1) / GSIZE
    return (rewards - centre) / jnp.maximum(jnp.sqrt(spread), REWARD_FLOOR)


def policy_terms(advantage, log_ratio):
    ratios = jnp.exp(log_ratio)
    plain = ratios * advantage[None, :]
    bounded = jnp.clip(ratios, 1.0 - CLIP_RANGE, 1.0 + CLIP_RANGE) * advantage[None, :]
    count = 2.0 * advantage.shape[0]
    loss_value = -jnp.sum(jnp.minimum(plain, bounded)) / count
    coef = jnp.where(plain <= bounded, -plain / count, jnp.float32(0.0))
    return (loss_value, coef)


def gather_all_to_all(x, axis_name, size):
    spread = jnp.broadcast_to(x[None], (size,) + x.shape)
    return lax.all_to_all(spread, axis_name, 0, 0, tiled=True)


def gather_pair(x, axis_name):
    other = lax.ppermute(x, axis_name, [(0, 1), (1, 0)])
    first = lax.axis_index(axis_name) == 0
    return jnp.where(first, jnp.stack([x, other]), jnp.stack([other, x]))


def reduce_pair(x, axis_name):
    me = lax.axis_index(axis_name)
    keep = lax.dynamic_index_in_dim(x, me, 0, keepdims=False)
    send = lax.dynamic_index_in_dim(x, 1 - me, 0, keepdims=False)
    sent = lax.ppermute(send.astype(jnp.bfloat16), axis_name, [(0, 1), (1, 0)])
    return keep + sent.astype(keep.dtype)


def on_device(
    latents,
    step_noise,
    ada_table,
    qkv_weight,
    out_weight,
    rewards,
    group_ids,
    time_index,
    log_ratio,
    z_size,
    seq_size,
):
    units = qkv_weight.shape[0] * qkv_weight.shape[1]
    qkv_t = jnp.transpose(qkv_weight, (2, 0, 1)).reshape(qkv_weight.shape[2], units)
    qkv_t = lax.all_gather(qkv_t, "z", axis=0, tiled=True)
    qkv_t = gather_pair(qkv_t, "xh").reshape(-1, units)
    projection_t = gather_pair(qkv_t, "grp").reshape(-1, units)
    out_rows = gather_all_to_all(out_weight, "z", z_size).reshape(-1, out_weight.shape[1])
    out_rows = gather_pair(out_rows, "xh").reshape(-1, out_weight.shape[1])
    out_rows = gather_pair(out_rows, "grp").reshape(-1, out_weight.shape[1])

    group_width = qkv_weight.shape[1]
    heads_here = group_width // HD
    samples = rewards.shape[0]
    seq_len = latents.shape[1]
    block_rows = min(512, seq_len)
    advantage = advantages(rewards, group_ids)
    loss_value, coef = policy_terms(advantage, log_ratio)
    my_index = lax.axis_index(SAMPLE_AXES)
    chooser = (jnp.arange(samples, dtype=jnp.int32) == my_index).astype(jnp.float32)
    my_coef = jnp.sum(coef * chooser[None, :], 1)
    step_size = 1.0 / TSTEPS
    state = latents[0]
    attn_list = []
    score_list = []
    plan = jnp.arange(TSTEPS, dtype=jnp.int32)
    blocks = gather_all_to_all(state, FEATURE_AXES, seq_size)
    whole = jnp.transpose(blocks, (1, 0, 2)).reshape(seq_len, -1)
    noise_blocks = gather_all_to_all(step_noise[0, 0], FEATURE_AXES, seq_size)
    for section in range(2):
        index_now = time_index[0] + section
        time_now = 1.0 - index_now.astype(jnp.float32) / TSTEPS
        picker = (plan == index_now).astype(jnp.float32)
        modulate = jnp.sum(picker[:, None, None] * ada_table, 0)
        centre = jnp.mean(whole, -1, keepdims=True)
        spread = jnp.mean((whole - centre) ** 2, -1, keepdims=True)
        normed = (
            (whole - centre) * lax.rsqrt(spread + NORM_EPS) * (1.0 + modulate[0][None, :])
            + modulate[1][None, :]
        ).astype(jnp.bfloat16)
        proj_rows = jnp.dot(normed, projection_t, preferred_element_type=jnp.float32).astype(
            jnp.bfloat16
        )
        proj_rows = proj_rows.reshape(seq_len, 3, heads_here, HD)
        key_rows = proj_rows[:, 1]
        value_rows = proj_rows[:, 2]
        query_rows = proj_rows[0:block_rows, 0]
        logits = jnp.einsum(
            "qhe,khe->hqk", query_rows, key_rows, preferred_element_type=jnp.float32
        ) * HD ** (-0.5)
        logits = logits - jnp.max(logits, -1, keepdims=True)
        weights = jnp.exp(logits)
        probs = (weights / jnp.sum(weights, -1, keepdims=True)).astype(jnp.bfloat16)
        attn_blocks = jnp.einsum(
            "hqk,khe->qhe", probs, value_rows, preferred_element_type=jnp.float32
        ).astype(jnp.bfloat16)
        attn = attn_blocks.reshape(seq_len, group_width)
        attn_parts = gather_all_to_all(attn, FEATURE_AXES, seq_size)
        attn_all = jnp.transpose(attn_parts, (1, 0, 2)).reshape(seq_len, -1)
        velocity = jnp.dot(attn_all, out_rows, preferred_element_type=jnp.float32)
        noise_level = SDE_NOISE * SDE_NOISE * time_now / (1.0 - time_now)
        std_dev = jnp.sqrt(noise_level * step_size)
        drift = velocity + noise_level / (2.0 * time_now) * (state + (1.0 - time_now) * velocity)
        mean_next = state - step_size * drift
        noise_now = step_noise[section, 0].astype(jnp.float32)
        state = mean_next + std_dev * noise_now
        if section == 0:
            vel_parts = gather_all_to_all(velocity.astype(jnp.bfloat16), FEATURE_AXES, seq_size)
            vel_whole = jnp.transpose(vel_parts, (1, 0, 2)).reshape(seq_len, -1).astype(jnp.float32)
            noise_whole = jnp.transpose(noise_blocks, (1, 0, 2)).reshape(seq_len, -1).astype(jnp.float32)
            drift_whole = vel_whole + noise_level / (2.0 * time_now) * (
                whole + (1.0 - time_now) * vel_whole
            )
            whole = whole - step_size * drift_whole + std_dev * noise_whole
        factor = (
            my_coef[section]
            * -step_size
            * (1.0 + noise_level * (1.0 - time_now) / (2.0 * time_now))
            / std_dev
        )
        score_list.append((factor * noise_now).astype(jnp.bfloat16))
        attn_list.append(attn_all)
    attn_both = jnp.stack(attn_list, 0)
    score_both = jnp.stack(score_list, 0)
    gradient = lax.dot_general(
        attn_both, score_both, (((0, 1), (0, 1)), ((), ())), preferred_element_type=jnp.float32
    )
    rows = gradient.shape[0]
    part = gradient.reshape(2, rows // 2, -1)
    part = reduce_pair(part, "grp")
    part = part.reshape(2, rows // 4, -1)
    part = reduce_pair(part, "xh")
    part = part.reshape(z_size, rows // (4 * z_size), -1)
    part = lax.all_to_all(part.astype(jnp.bfloat16), "z", 0, 0, tiled=True)
    out_grad = jnp.sum(part.astype(jnp.float32), 0)
    return (state[None], loss_value, out_grad)


def solution(mesh):
    grp, dp, seq = (mesh.shape[a] for a in ("grp", "dp", "seq"))
    xh, xl = 2, 2
    z_size, y_size = dp // xh, seq // xl
    fine = Mesh(
        mesh.devices.reshape(grp, xh, z_size, y_size, xl), ("grp", "xh", "z", "y", "xl")
    )
    samples = SAMPLE_AXES
    features = FEATURE_AXES

    def body(*args):
        return on_device(*args, z_size=z_size, seq_size=seq)

    return jax.shard_map(
        body,
        mesh=fine,
        in_specs=(
            P(samples, None, features),
            P(None, samples, None, features),
            P(),
            P(None, features, samples),
            P(samples, features),
            P(),
            P(),
            P(samples),
            P(),
        ),
        out_specs=(P(samples, None, features), P(), P(samples, features)),
        check_vma=False,
    )
```

```python
import jax
import jax.numpy as jnp
from jax import lax
from jax.sharding import Mesh
from jax.sharding import PartitionSpec as P

HD = 64
TSTEPS = 10
GSIZE = 8


SDE_NOISE = 0.7
CLIP_RANGE = 0.2
REWARD_FLOOR = 0.75
NORM_EPS = 1e-06

SAMPLE_AXES = ("grp", "xh", "z")
FEATURE_AXES = ("y", "xl")


def advantages(rewards, group_ids):
    same_group = (group_ids[:, None] == group_ids[None, :]).astype(jnp.float32)
    centre = jnp.sum(same_group * rewards[None, :], 1) / GSIZE
    spread = jnp.sum(same_group * (rewards[None, :] - centre[:, None]) ** 2, 1) / GSIZE
    return (rewards - centre) / jnp.maximum(jnp.sqrt(spread), REWARD_FLOOR)


def policy_terms(advantage, log_ratio):
    ratios = jnp.exp(log_ratio)
    plain = ratios * advantage[None, :]
    bounded = jnp.clip(ratios, 1.0 - CLIP_RANGE, 1.0 + CLIP_RANGE) * advantage[None, :]
    count = 2.0 * advantage.shape[0]
    loss_value = -jnp.sum(jnp.minimum(plain, bounded)) / count
    coef = jnp.where(plain <= bounded, -plain / count, jnp.float32(0.0))
    return (loss_value, coef)


def gather_all_to_all(x, axis_name, size):
    spread = jnp.broadcast_to(x[None], (size,) + x.shape)
    return lax.all_to_all(spread, axis_name, 0, 0, tiled=True)


def gather_pair(x, axis_name):
    other = lax.ppermute(x, axis_name, [(0, 1), (1, 0)])
    first = lax.axis_index(axis_name) == 0
    return jnp.where(first, jnp.stack([x, other]), jnp.stack([other, x]))


def reduce_pair(x, axis_name):
    me = lax.axis_index(axis_name)
    keep = lax.dynamic_index_in_dim(x, me, 0, keepdims=False)
    send = lax.dynamic_index_in_dim(x, 1 - me, 0, keepdims=False)
    sent = lax.ppermute(send.astype(jnp.bfloat16), axis_name, [(0, 1), (1, 0)])
    return keep + sent.astype(keep.dtype)


def on_device(
    latents,
    step_noise,
    ada_table,
    qkv_weight,
    out_weight,
    rewards,
    group_ids,
    time_index,
    log_ratio,
    z_size,
    seq_size,
):
    units = qkv_weight.shape[0] * qkv_weight.shape[1]
    qkv_t = jnp.transpose(qkv_weight, (2, 0, 1)).reshape(qkv_weight.shape[2], units)
    out_rows = gather_all_to_all(out_weight, "z", z_size).reshape(-1, out_weight.shape[1])
    out_rows, latents, qkv_t = lax.optimization_barrier((out_rows, latents, qkv_t))
    qkv_t = lax.all_gather(qkv_t, "z", axis=0, tiled=True)
    qkv_t = gather_pair(qkv_t, "xh").reshape(-1, units)
    projection_t = gather_pair(qkv_t, "grp").reshape(-1, units)
    out_rows = gather_pair(out_rows, "xh").reshape(-1, out_weight.shape[1])
    out_rows = gather_pair(out_rows, "grp").reshape(-1, out_weight.shape[1])

    group_width = qkv_weight.shape[1]
    heads_here = group_width // HD
    samples = rewards.shape[0]
    seq_len = latents.shape[1]
    block_rows = min(512, seq_len)
    advantage = advantages(rewards, group_ids)
    loss_value, coef = policy_terms(advantage, log_ratio)
    my_index = lax.axis_index(SAMPLE_AXES)
    chooser = (jnp.arange(samples, dtype=jnp.int32) == my_index).astype(jnp.float32)
    my_coef = jnp.sum(coef * chooser[None, :], 1)
    step_size = 1.0 / TSTEPS
    state = latents[0]
    attn_list = []
    score_list = []
    plan = jnp.arange(TSTEPS, dtype=jnp.int32)
    for section in range(2):
        index_now = time_index[0] + section
        time_now = 1.0 - index_now.astype(jnp.float32) / TSTEPS
        picker = (plan == index_now).astype(jnp.float32)
        modulate = jnp.sum(picker[:, None, None] * ada_table, 0)
        blocks = gather_all_to_all(state, FEATURE_AXES, seq_size)
        whole = jnp.transpose(blocks, (1, 0, 2)).reshape(seq_len, -1)
        centre = jnp.mean(whole, -1, keepdims=True)
        spread = jnp.mean((whole - centre) ** 2, -1, keepdims=True)
        normed = (
            (whole - centre) * lax.rsqrt(spread + NORM_EPS) * (1.0 + modulate[0][None, :])
            + modulate[1][None, :]
        ).astype(jnp.bfloat16)
        proj_rows = jnp.dot(normed, projection_t, preferred_element_type=jnp.float32).astype(
            jnp.bfloat16
        )
        proj_rows = proj_rows.reshape(seq_len, 3, heads_here, HD)
        key_rows = proj_rows[:, 1]
        value_rows = proj_rows[:, 2]
        query_rows = proj_rows[0:block_rows, 0]
        logits = jnp.einsum(
            "qhe,khe->hqk", query_rows, key_rows, preferred_element_type=jnp.float32
        ) * HD ** (-0.5)
        logits = logits - jnp.max(logits, -1, keepdims=True)
        weights = jnp.exp(logits)
        probs = (weights / jnp.sum(weights, -1, keepdims=True)).astype(jnp.bfloat16)
        attn_blocks = jnp.einsum(
            "hqk,khe->qhe", probs, value_rows, preferred_element_type=jnp.float32
        ).astype(jnp.bfloat16)
        attn = attn_blocks.reshape(seq_len, group_width)
        attn_parts = gather_all_to_all(attn, FEATURE_AXES, seq_size)
        attn_all = jnp.transpose(attn_parts, (1, 0, 2)).reshape(seq_len, -1)
        velocity = jnp.dot(attn_all, out_rows, preferred_element_type=jnp.float32)
        noise_level = SDE_NOISE * SDE_NOISE * time_now / (1.0 - time_now)
        std_dev = jnp.sqrt(noise_level * step_size)
        drift = velocity + noise_level / (2.0 * time_now) * (state + (1.0 - time_now) * velocity)
        mean_next = state - step_size * drift
        noise_now = step_noise[section, 0].astype(jnp.float32)
        state = mean_next + std_dev * noise_now
        factor = (
            my_coef[section]
            * -step_size
            * (1.0 + noise_level * (1.0 - time_now) / (2.0 * time_now))
            / std_dev
        )
        score_list.append((factor * noise_now).astype(jnp.bfloat16))
        attn_list.append(attn_all)
    attn_both = jnp.stack(attn_list, 0)
    score_both = jnp.stack(score_list, 0)
    rows = attn_both.shape[2]
    attn_halves = attn_both.reshape(attn_both.shape[0], attn_both.shape[1], 2, rows // 2)
    part = lax.dot_general(
        attn_halves, score_both, (((0, 1), (0, 1)), ((), ())), preferred_element_type=jnp.float32
    )
    part = reduce_pair(part, "grp")
    part = part.reshape(2, rows // 4, -1)
    part = reduce_pair(part, "xh")
    part = part.reshape(z_size, rows // (4 * z_size), -1)
    part = lax.all_to_all(part.astype(jnp.bfloat16), "z", 0, 0, tiled=True)
    out_grad = jnp.sum(part.astype(jnp.float32), 0)
    return (state[None], loss_value, out_grad)


def solution(mesh):
    grp, dp, seq = (mesh.shape[a] for a in ("grp", "dp", "seq"))
    xh, xl = 2, 2
    z_size, y_size = dp // xh, seq // xl
    fine = Mesh(
        mesh.devices.reshape(grp, xh, z_size, y_size, xl), ("grp", "xh", "z", "y", "xl")
    )
    samples = SAMPLE_AXES
    features = FEATURE_AXES

    def body(*args):
        return on_device(*args, z_size=z_size, seq_size=seq)

    return jax.shard_map(
        body,
        mesh=fine,
        in_specs=(
            P(samples, None, features),
            P(None, samples, None, features),
            P(),
            P(None, features, samples),
            P(samples, features),
            P(),
            P(),
            P(samples),
            P(),
        ),
        out_specs=(P(samples, None, features), P(), P(samples, features)),
        check_vma=False,
    )
```

```python
import jax
import jax.numpy as jnp
from jax import lax
from jax.sharding import Mesh
from jax.sharding import PartitionSpec as P

HD = 64
TSTEPS = 10
GSIZE = 8


SDE_NOISE = 0.7
CLIP_RANGE = 0.2
REWARD_FLOOR = 0.75
NORM_EPS = 1e-06

SAMPLE_AXES = ("grp", "xh", "z")
FEATURE_AXES = ("y", "xl")


def advantages(rewards, group_ids):
    same_group = (group_ids[:, None] == group_ids[None, :]).astype(jnp.float32)
    centre = jnp.sum(same_group * rewards[None, :], 1) / GSIZE
    spread = jnp.sum(same_group * (rewards[None, :] - centre[:, None]) ** 2, 1) / GSIZE
    return (rewards - centre) / jnp.maximum(jnp.sqrt(spread), REWARD_FLOOR)


def policy_terms(advantage, log_ratio):
    ratios = jnp.exp(log_ratio)
    plain = ratios * advantage[None, :]
    bounded = jnp.clip(ratios, 1.0 - CLIP_RANGE, 1.0 + CLIP_RANGE) * advantage[None, :]
    count = 2.0 * advantage.shape[0]
    loss_value = -jnp.sum(jnp.minimum(plain, bounded)) / count
    coef = jnp.where(plain <= bounded, -plain / count, jnp.float32(0.0))
    return (loss_value, coef)


def gather_all_to_all(x, axis_name, size):
    spread = jnp.broadcast_to(x[None], (size,) + x.shape)
    return lax.all_to_all(spread, axis_name, 0, 0, tiled=True)


def gather_pair(x, axis_name):
    other = lax.ppermute(x, axis_name, [(0, 1), (1, 0)])
    first = lax.axis_index(axis_name) == 0
    return jnp.where(first, jnp.stack([x, other]), jnp.stack([other, x]))


def reduce_pair(x, axis_name):
    me = lax.axis_index(axis_name)
    keep = lax.dynamic_index_in_dim(x, me, 0, keepdims=False)
    send = lax.dynamic_index_in_dim(x, 1 - me, 0, keepdims=False)
    sent = lax.ppermute(send.astype(jnp.bfloat16), axis_name, [(0, 1), (1, 0)])
    return keep + sent.astype(keep.dtype)


def on_device(
    latents,
    step_noise,
    ada_table,
    qkv_weight,
    out_weight,
    rewards,
    group_ids,
    time_index,
    log_ratio,
    z_size,
    seq_size,
):
    units = qkv_weight.shape[0] * qkv_weight.shape[1]
    qkv_t = jnp.transpose(qkv_weight, (2, 0, 1)).reshape(qkv_weight.shape[2], units)
    qkv_t = lax.all_gather(qkv_t, "z", axis=0, tiled=True)
    qkv_t = gather_pair(qkv_t, "xh").reshape(-1, units)
    projection_t = gather_pair(qkv_t, "grp").reshape(-1, units)
    first_blocks = gather_all_to_all(latents[0].astype(jnp.bfloat16), FEATURE_AXES, seq_size)
    first_blocks, out_weight = lax.optimization_barrier((first_blocks, out_weight))
    out_rows = gather_all_to_all(out_weight, "z", z_size).reshape(-1, out_weight.shape[1])
    out_rows = gather_pair(out_rows, "xh").reshape(-1, out_weight.shape[1])
    out_rows = gather_pair(out_rows, "grp").reshape(-1, out_weight.shape[1])

    group_width = qkv_weight.shape[1]
    heads_here = group_width // HD
    samples = rewards.shape[0]
    seq_len = latents.shape[1]
    block_rows = min(512, seq_len)
    advantage = advantages(rewards, group_ids)
    loss_value, coef = policy_terms(advantage, log_ratio)
    my_index = lax.axis_index(SAMPLE_AXES)
    chooser = (jnp.arange(samples, dtype=jnp.int32) == my_index).astype(jnp.float32)
    my_coef = jnp.sum(coef * chooser[None, :], 1)
    step_size = 1.0 / TSTEPS
    state = latents[0]
    attn_list = []
    score_list = []
    plan = jnp.arange(TSTEPS, dtype=jnp.int32)
    for section in range(2):
        index_now = time_index[0] + section
        time_now = 1.0 - index_now.astype(jnp.float32) / TSTEPS
        picker = (plan == index_now).astype(jnp.float32)
        modulate = jnp.sum(picker[:, None, None] * ada_table, 0)
        if section == 0:
            blocks = first_blocks
        else:
            blocks = gather_all_to_all(state.astype(jnp.bfloat16), FEATURE_AXES, seq_size)
        whole = jnp.transpose(blocks, (1, 0, 2)).reshape(seq_len, -1).astype(jnp.float32)
        centre = jnp.mean(whole, -1, keepdims=True)
        spread = jnp.mean((whole - centre) ** 2, -1, keepdims=True)
        normed = (
            (whole - centre) * lax.rsqrt(spread + NORM_EPS) * (1.0 + modulate[0][None, :])
            + modulate[1][None, :]
        ).astype(jnp.bfloat16)
        proj_rows = jnp.dot(normed, projection_t, preferred_element_type=jnp.float32).astype(
            jnp.bfloat16
        )
        proj_rows = proj_rows.reshape(seq_len, 3, heads_here, HD)
        key_rows = proj_rows[:, 1]
        value_rows = proj_rows[:, 2]
        query_rows = proj_rows[0:block_rows, 0]
        logits = jnp.einsum(
            "qhe,khe->hqk", query_rows, key_rows, preferred_element_type=jnp.float32
        ) * HD ** (-0.5)
        logits = logits - jnp.max(logits, -1, keepdims=True)
        weights = jnp.exp(logits)
        probs = (weights / jnp.sum(weights, -1, keepdims=True)).astype(jnp.bfloat16)
        attn_blocks = jnp.einsum(
            "hqk,khe->qhe", probs, value_rows, preferred_element_type=jnp.float32
        ).astype(jnp.bfloat16)
        attn = attn_blocks.reshape(seq_len, group_width)
        attn_parts = gather_all_to_all(attn, FEATURE_AXES, seq_size)
        attn_all = jnp.transpose(attn_parts, (1, 0, 2)).reshape(seq_len, -1)
        velocity = jnp.dot(attn_all, out_rows, preferred_element_type=jnp.float32)
        noise_level = SDE_NOISE * SDE_NOISE * time_now / (1.0 - time_now)
        std_dev = jnp.sqrt(noise_level * step_size)
        drift = velocity + noise_level / (2.0 * time_now) * (state + (1.0 - time_now) * velocity)
        mean_next = state - step_size * drift
        noise_now = step_noise[section, 0].astype(jnp.float32)
        state = mean_next + std_dev * noise_now
        factor = (
            my_coef[section]
            * -step_size
            * (1.0 + noise_level * (1.0 - time_now) / (2.0 * time_now))
            / std_dev
        )
        score_list.append((factor * noise_now).astype(jnp.bfloat16))
        attn_list.append(attn_all)
    attn_both = jnp.stack(attn_list, 0)
    score_both = jnp.stack(score_list, 0)
    gradient = lax.dot_general(
        attn_both, score_both, (((0, 1), (0, 1)), ((), ())), preferred_element_type=jnp.float32
    )
    rows = gradient.shape[0]
    part = gradient.reshape(2, rows // 2, -1)
    part = reduce_pair(part, "grp")
    part = part.reshape(2, rows // 4, -1)
    part = reduce_pair(part, "xh")
    part = part.reshape(z_size, rows // (4 * z_size), -1)
    part = lax.all_to_all(part.astype(jnp.bfloat16), "z", 0, 0, tiled=True)
    out_grad = jnp.sum(part.astype(jnp.float32), 0)
    return (state[None], loss_value, out_grad)


def solution(mesh):
    grp, dp, seq = (mesh.shape[a] for a in ("grp", "dp", "seq"))
    xh, xl = 2, 2
    z_size, y_size = dp // xh, seq // xl
    fine = Mesh(
        mesh.devices.reshape(grp, xh, z_size, y_size, xl), ("grp", "xh", "z", "y", "xl")
    )
    samples = SAMPLE_AXES
    features = FEATURE_AXES

    def body(*args):
        return on_device(*args, z_size=z_size, seq_size=seq)

    return jax.shard_map(
        body,
        mesh=fine,
        in_specs=(
            P(samples, None, features),
            P(None, samples, None, features),
            P(),
            P(None, features, samples),
            P(samples, features),
            P(),
            P(),
            P(samples),
            P(),
        ),
        out_specs=(P(samples, None, features), P(), P(samples, features)),
        check_vma=False,
    )
```

```python
import jax
import jax.numpy as jnp
from jax import lax
from jax.sharding import Mesh
from jax.sharding import PartitionSpec as P

HD = 64
TSTEPS = 10
GSIZE = 8


SDE_NOISE = 0.7
CLIP_RANGE = 0.2
REWARD_FLOOR = 0.75
NORM_EPS = 1e-06

SAMPLE_AXES = ("grp", "xh", "z")
FEATURE_AXES = ("y", "xl")


def advantages(rewards, group_ids):
    same_group = (group_ids[:, None] == group_ids[None, :]).astype(jnp.float32)
    centre = jnp.sum(same_group * rewards[None, :], 1) / GSIZE
    spread = jnp.sum(same_group * (rewards[None, :] - centre[:, None]) ** 2, 1) / GSIZE
    return (rewards - centre) / jnp.maximum(jnp.sqrt(spread), REWARD_FLOOR)


def policy_terms(advantage, log_ratio):
    ratios = jnp.exp(log_ratio)
    plain = ratios * advantage[None, :]
    bounded = jnp.clip(ratios, 1.0 - CLIP_RANGE, 1.0 + CLIP_RANGE) * advantage[None, :]
    count = 2.0 * advantage.shape[0]
    loss_value = -jnp.sum(jnp.minimum(plain, bounded)) / count
    coef = jnp.where(plain <= bounded, -plain / count, jnp.float32(0.0))
    return (loss_value, coef)


def gather_all_to_all(x, axis_name, size):
    spread = jnp.broadcast_to(x[None], (size,) + x.shape)
    return lax.all_to_all(spread, axis_name, 0, 0, tiled=True)


def gather_pair(x, axis_name):
    other = lax.ppermute(x, axis_name, [(0, 1), (1, 0)])
    first = lax.axis_index(axis_name) == 0
    return jnp.where(first, jnp.stack([x, other]), jnp.stack([other, x]))


def reduce_pair(x, axis_name):
    me = lax.axis_index(axis_name)
    keep = lax.dynamic_index_in_dim(x, me, 0, keepdims=False)
    send = lax.dynamic_index_in_dim(x, 1 - me, 0, keepdims=False)
    sent = lax.ppermute(send.astype(jnp.bfloat16), axis_name, [(0, 1), (1, 0)])
    return keep + sent.astype(keep.dtype)


def on_device(
    latents,
    step_noise,
    ada_table,
    qkv_weight,
    out_weight,
    rewards,
    group_ids,
    time_index,
    log_ratio,
    z_size,
    seq_size,
):
    units = qkv_weight.shape[0] * qkv_weight.shape[1]
    qkv_t = jnp.transpose(qkv_weight, (2, 0, 1)).reshape(qkv_weight.shape[2], units)
    qkv_t = lax.all_gather(qkv_t, "z", axis=0, tiled=True)
    qkv_t = gather_pair(qkv_t, "xh").reshape(-1, units)
    projection_t = gather_pair(qkv_t, "grp").reshape(-1, units)
    first_blocks = gather_all_to_all(latents[0].astype(jnp.bfloat16), FEATURE_AXES, seq_size)
    out_shape = out_weight.shape
    projection_t, out_weight = lax.optimization_barrier((projection_t, out_weight))
    out_z = gather_all_to_all(out_weight, "z", z_size).reshape(-1, out_shape[1])

    group_width = qkv_weight.shape[1]
    heads_here = group_width // HD
    samples = rewards.shape[0]
    seq_len = latents.shape[1]
    block_rows = min(512, seq_len)
    advantage = advantages(rewards, group_ids)
    loss_value, coef = policy_terms(advantage, log_ratio)
    my_index = lax.axis_index(SAMPLE_AXES)
    chooser = (jnp.arange(samples, dtype=jnp.int32) == my_index).astype(jnp.float32)
    my_coef = jnp.sum(coef * chooser[None, :], 1)
    step_size = 1.0 / TSTEPS
    state = latents[0]
    attn_list = []
    score_list = []
    plan = jnp.arange(TSTEPS, dtype=jnp.int32)
    for section in range(2):
        index_now = time_index[0] + section
        time_now = 1.0 - index_now.astype(jnp.float32) / TSTEPS
        picker = (plan == index_now).astype(jnp.float32)
        modulate = jnp.sum(picker[:, None, None] * ada_table, 0)
        if section == 0:
            blocks = first_blocks
        else:
            blocks = gather_all_to_all(state.astype(jnp.bfloat16), FEATURE_AXES, seq_size)
        whole = jnp.transpose(blocks, (1, 0, 2)).reshape(seq_len, -1).astype(jnp.float32)
        centre = jnp.mean(whole, -1, keepdims=True)
        spread = jnp.mean((whole - centre) ** 2, -1, keepdims=True)
        normed = (
            (whole - centre) * lax.rsqrt(spread + NORM_EPS) * (1.0 + modulate[0][None, :])
            + modulate[1][None, :]
        ).astype(jnp.bfloat16)
        proj_rows = jnp.dot(normed, projection_t, preferred_element_type=jnp.float32).astype(
            jnp.bfloat16
        )
        proj_rows = proj_rows.reshape(seq_len, 3, heads_here, HD)
        key_rows = proj_rows[:, 1]
        value_rows = proj_rows[:, 2]
        query_rows = proj_rows[0:block_rows, 0]
        logits = jnp.einsum(
            "qhe,khe->hqk", query_rows, key_rows, preferred_element_type=jnp.float32
        ) * HD ** (-0.5)
        logits = logits - jnp.max(logits, -1, keepdims=True)
        weights = jnp.exp(logits)
        probs = (weights / jnp.sum(weights, -1, keepdims=True)).astype(jnp.bfloat16)
        attn_blocks = jnp.einsum(
            "hqk,khe->qhe", probs, value_rows, preferred_element_type=jnp.float32
        ).astype(jnp.bfloat16)
        attn = attn_blocks.reshape(seq_len, group_width)
        if section == 0:
            out_z, attn = lax.optimization_barrier((out_z, attn))
            out_rows = gather_pair(out_z, "xh").reshape(-1, out_shape[1])
            out_rows = gather_pair(out_rows, "grp").reshape(-1, out_shape[1])
        attn_parts = gather_all_to_all(attn, FEATURE_AXES, seq_size)
        attn_all = jnp.transpose(attn_parts, (1, 0, 2)).reshape(seq_len, -1)
        velocity = jnp.dot(attn_all, out_rows, preferred_element_type=jnp.float32)
        noise_level = SDE_NOISE * SDE_NOISE * time_now / (1.0 - time_now)
        std_dev = jnp.sqrt(noise_level * step_size)
        drift = velocity + noise_level / (2.0 * time_now) * (state + (1.0 - time_now) * velocity)
        mean_next = state - step_size * drift
        noise_now = step_noise[section, 0].astype(jnp.float32)
        state = mean_next + std_dev * noise_now
        factor = (
            my_coef[section]
            * -step_size
            * (1.0 + noise_level * (1.0 - time_now) / (2.0 * time_now))
            / std_dev
        )
        score_list.append((factor * noise_now).astype(jnp.bfloat16))
        attn_list.append(attn_all)
    attn_both = jnp.stack(attn_list, 0)
    score_both = jnp.stack(score_list, 0)
    gradient = lax.dot_general(
        attn_both, score_both, (((0, 1), (0, 1)), ((), ())), preferred_element_type=jnp.float32
    )
    rows = gradient.shape[0]
    part = gradient.reshape(2, rows // 2, -1)
    part = reduce_pair(part, "grp")
    part = part.reshape(2 * z_size, rows // (4 * z_size), -1)
    part = lax.all_to_all(part.astype(jnp.bfloat16), ("xh", "z"), 0, 0, tiled=True)
    out_grad = jnp.sum(part.astype(jnp.float32), 0)
    return (state[None], loss_value, out_grad)


def solution(mesh):
    grp, dp, seq = (mesh.shape[a] for a in ("grp", "dp", "seq"))
    xh, xl = 2, 2
    z_size, y_size = dp // xh, seq // xl
    fine = Mesh(
        mesh.devices.reshape(grp, xh, z_size, y_size, xl), ("grp", "xh", "z", "y", "xl")
    )
    samples = SAMPLE_AXES
    features = FEATURE_AXES

    def body(*args):
        return on_device(*args, z_size=z_size, seq_size=seq)

    return jax.shard_map(
        body,
        mesh=fine,
        in_specs=(
            P(samples, None, features),
            P(None, samples, None, features),
            P(),
            P(None, features, samples),
            P(samples, features),
            P(),
            P(),
            P(samples),
            P(),
        ),
        out_specs=(P(samples, None, features), P(), P(samples, features)),
        check_vma=False,
    )
```

```python
import jax
import jax.numpy as jnp
from jax import lax
from jax.sharding import Mesh
from jax.sharding import PartitionSpec as P

HD = 64
TSTEPS = 10
GSIZE = 8


SDE_NOISE = 0.7
CLIP_RANGE = 0.2
REWARD_FLOOR = 0.75
NORM_EPS = 1e-06

SAMPLE_AXES = ("grp", "xh", "z")
FEATURE_AXES = ("y", "xl")


def advantages(rewards, group_ids):
    same_group = (group_ids[:, None] == group_ids[None, :]).astype(jnp.float32)
    centre = jnp.sum(same_group * rewards[None, :], 1) / GSIZE
    spread = jnp.sum(same_group * (rewards[None, :] - centre[:, None]) ** 2, 1) / GSIZE
    return (rewards - centre) / jnp.maximum(jnp.sqrt(spread), REWARD_FLOOR)


def policy_terms(advantage, log_ratio):
    ratios = jnp.exp(log_ratio)
    plain = ratios * advantage[None, :]
    bounded = jnp.clip(ratios, 1.0 - CLIP_RANGE, 1.0 + CLIP_RANGE) * advantage[None, :]
    count = 2.0 * advantage.shape[0]
    loss_value = -jnp.sum(jnp.minimum(plain, bounded)) / count
    coef = jnp.where(plain <= bounded, -plain / count, jnp.float32(0.0))
    return (loss_value, coef)


def gather_all_to_all(x, axis_name, size):
    spread = jnp.broadcast_to(x[None], (size,) + x.shape)
    return lax.all_to_all(spread, axis_name, 0, 0, tiled=True)


def gather_pair(x, axis_name):
    other = lax.ppermute(x, axis_name, [(0, 1), (1, 0)])
    first = lax.axis_index(axis_name) == 0
    return jnp.where(first, jnp.stack([x, other]), jnp.stack([other, x]))


def reduce_pair(x, axis_name):
    me = lax.axis_index(axis_name)
    keep = lax.dynamic_index_in_dim(x, me, 0, keepdims=False)
    send = lax.dynamic_index_in_dim(x, 1 - me, 0, keepdims=False)
    sent = lax.ppermute(send.astype(jnp.bfloat16), axis_name, [(0, 1), (1, 0)])
    return keep + sent.astype(keep.dtype)


def on_device(
    latents,
    step_noise,
    ada_table,
    qkv_weight,
    out_weight,
    rewards,
    group_ids,
    time_index,
    log_ratio,
    z_size,
    seq_size,
):
    units = qkv_weight.shape[0] * qkv_weight.shape[1]
    width_rows = qkv_weight.shape[2]
    out_shape = out_weight.shape
    qkv_t = jnp.transpose(qkv_weight, (2, 0, 1)).reshape(width_rows, units)
    qkv_z = lax.all_gather(qkv_t, "z", axis=0, tiled=True)
    out_z = lax.all_gather(out_weight, "z", axis=0, tiled=True)
    both = jnp.concatenate([qkv_z, out_z.reshape(qkv_z.shape[0], -1)], axis=1)
    both = gather_pair(both, "xh").reshape(-1, both.shape[1])
    both = gather_pair(both, "grp").reshape(-1, both.shape[1])
    projection_t = both[:, :units]
    out_rows = both[:, units:].reshape(-1, out_shape[1])
    first_blocks = gather_all_to_all(latents[0].astype(jnp.bfloat16), FEATURE_AXES, seq_size)

    group_width = qkv_weight.shape[1]
    heads_here = group_width // HD
    samples = rewards.shape[0]
    seq_len = latents.shape[1]
    block_rows = min(512, seq_len)
    advantage = advantages(rewards, group_ids)
    loss_value, coef = policy_terms(advantage, log_ratio)
    my_index = lax.axis_index(SAMPLE_AXES)
    chooser = (jnp.arange(samples, dtype=jnp.int32) == my_index).astype(jnp.float32)
    my_coef = jnp.sum(coef * chooser[None, :], 1)
    step_size = 1.0 / TSTEPS
    state = latents[0]
    attn_list = []
    score_list = []
    plan = jnp.arange(TSTEPS, dtype=jnp.int32)
    for section in range(2):
        index_now = time_index[0] + section
        time_now = 1.0 - index_now.astype(jnp.float32) / TSTEPS
        picker = (plan == index_now).astype(jnp.float32)
        modulate = jnp.sum(picker[:, None, None] * ada_table, 0)
        if section == 0:
            blocks = first_blocks
        else:
            blocks = gather_all_to_all(state.astype(jnp.bfloat16), FEATURE_AXES, seq_size)
        whole = jnp.transpose(blocks, (1, 0, 2)).reshape(seq_len, -1).astype(jnp.float32)
        centre = jnp.mean(whole, -1, keepdims=True)
        spread = jnp.mean((whole - centre) ** 2, -1, keepdims=True)
        normed = (
            (whole - centre) * lax.rsqrt(spread + NORM_EPS) * (1.0 + modulate[0][None, :])
            + modulate[1][None, :]
        ).astype(jnp.bfloat16)
        proj_rows = jnp.dot(normed, projection_t, preferred_element_type=jnp.float32).astype(
            jnp.bfloat16
        )
        proj_rows = proj_rows.reshape(seq_len, 3, heads_here, HD)
        key_rows = proj_rows[:, 1]
        value_rows = proj_rows[:, 2]
        query_rows = proj_rows[0:block_rows, 0]
        logits = jnp.einsum(
            "qhe,khe->hqk", query_rows, key_rows, preferred_element_type=jnp.float32
        ) * HD ** (-0.5)
        logits = logits - jnp.max(logits, -1, keepdims=True)
        weights = jnp.exp(logits)
        probs = (weights / jnp.sum(weights, -1, keepdims=True)).astype(jnp.bfloat16)
        attn_blocks = jnp.einsum(
            "hqk,khe->qhe", probs, value_rows, preferred_element_type=jnp.float32
        ).astype(jnp.bfloat16)
        attn = attn_blocks.reshape(seq_len, group_width)
        attn_parts = gather_all_to_all(attn, FEATURE_AXES, seq_size)
        attn_all = jnp.transpose(attn_parts, (1, 0, 2)).reshape(seq_len, -1)
        velocity = jnp.dot(attn_all, out_rows, preferred_element_type=jnp.float32)
        noise_level = SDE_NOISE * SDE_NOISE * time_now / (1.0 - time_now)
        std_dev = jnp.sqrt(noise_level * step_size)
        drift = velocity + noise_level / (2.0 * time_now) * (state + (1.0 - time_now) * velocity)
        mean_next = state - step_size * drift
        noise_now = step_noise[section, 0].astype(jnp.float32)
        state = mean_next + std_dev * noise_now
        factor = (
            my_coef[section]
            * -step_size
            * (1.0 + noise_level * (1.0 - time_now) / (2.0 * time_now))
            / std_dev
        )
        score_list.append((factor * noise_now).astype(jnp.bfloat16))
        attn_list.append(attn_all)
    attn_both = jnp.stack(attn_list, 0)
    score_both = jnp.stack(score_list, 0)
    gradient = lax.dot_general(
        attn_both, score_both, (((0, 1), (0, 1)), ((), ())), preferred_element_type=jnp.float32
    )
    rows = gradient.shape[0]
    part = gradient.reshape(2, rows // 2, -1)
    part = reduce_pair(part, "grp")
    part = part.reshape(2, rows // 4, -1)
    part = reduce_pair(part, "xh")
    part = part.reshape(z_size, rows // (4 * z_size), -1)
    part = lax.all_to_all(part.astype(jnp.bfloat16), "z", 0, 0, tiled=True)
    out_grad = jnp.sum(part.astype(jnp.float32), 0)
    return (state[None], loss_value, out_grad)


def solution(mesh):
    grp, dp, seq = (mesh.shape[a] for a in ("grp", "dp", "seq"))
    xh, xl = 2, 2
    z_size, y_size = dp // xh, seq // xl
    fine = Mesh(
        mesh.devices.reshape(grp, xh, z_size, y_size, xl), ("grp", "xh", "z", "y", "xl")
    )
    samples = SAMPLE_AXES
    features = FEATURE_AXES

    def body(*args):
        return on_device(*args, z_size=z_size, seq_size=seq)

    return jax.shard_map(
        body,
        mesh=fine,
        in_specs=(
            P(samples, None, features),
            P(None, samples, None, features),
            P(),
            P(None, features, samples),
            P(samples, features),
            P(),
            P(),
            P(samples),
            P(),
        ),
        out_specs=(P(samples, None, features), P(), P(samples, features)),
        check_vma=False,
    )
```

```python
import jax
import jax.numpy as jnp
from jax import lax
from jax.sharding import Mesh
from jax.sharding import PartitionSpec as P

HD = 64
TSTEPS = 10
GSIZE = 8


SDE_NOISE = 0.7
CLIP_RANGE = 0.2
REWARD_FLOOR = 0.75
NORM_EPS = 1e-06

SAMPLE_AXES = ("grp", "xh", "z")
FEATURE_AXES = ("y", "xl")


def advantages(rewards, group_ids):
    same_group = (group_ids[:, None] == group_ids[None, :]).astype(jnp.float32)
    centre = jnp.sum(same_group * rewards[None, :], 1) / GSIZE
    spread = jnp.sum(same_group * (rewards[None, :] - centre[:, None]) ** 2, 1) / GSIZE
    return (rewards - centre) / jnp.maximum(jnp.sqrt(spread), REWARD_FLOOR)


def policy_terms(advantage, log_ratio):
    ratios = jnp.exp(log_ratio)
    plain = ratios * advantage[None, :]
    bounded = jnp.clip(ratios, 1.0 - CLIP_RANGE, 1.0 + CLIP_RANGE) * advantage[None, :]
    count = 2.0 * advantage.shape[0]
    loss_value = -jnp.sum(jnp.minimum(plain, bounded)) / count
    coef = jnp.where(plain <= bounded, -plain / count, jnp.float32(0.0))
    return (loss_value, coef)


def gather_all_to_all(x, axis_name, size):
    spread = jnp.broadcast_to(x[None], (size,) + x.shape)
    return lax.all_to_all(spread, axis_name, 0, 0, tiled=True)


def gather_pair(x, axis_name):
    other = lax.ppermute(x, axis_name, [(0, 1), (1, 0)])
    first = lax.axis_index(axis_name) == 0
    return jnp.where(first, jnp.stack([x, other]), jnp.stack([other, x]))


def reduce_pair(x, axis_name):
    me = lax.axis_index(axis_name)
    keep = lax.dynamic_index_in_dim(x, me, 0, keepdims=False)
    send = lax.dynamic_index_in_dim(x, 1 - me, 0, keepdims=False)
    sent = lax.ppermute(send.astype(jnp.bfloat16), axis_name, [(0, 1), (1, 0)])
    return keep + sent.astype(keep.dtype)


def on_device(
    latents,
    step_noise,
    ada_table,
    qkv_weight,
    out_weight,
    rewards,
    group_ids,
    time_index,
    log_ratio,
    z_size,
    seq_size,
):
    units = qkv_weight.shape[0] * qkv_weight.shape[1]
    out_shape = out_weight.shape
    first_blocks = gather_all_to_all(latents[0].astype(jnp.bfloat16), FEATURE_AXES, seq_size)
    qkv_t = jnp.transpose(qkv_weight, (2, 0, 1)).reshape(qkv_weight.shape[2], units)
    first_blocks, qkv_t = lax.optimization_barrier((first_blocks, qkv_t))
    qkv_t = lax.all_gather(qkv_t, "z", axis=0, tiled=True)
    qkv_t, out_weight = lax.optimization_barrier((qkv_t, out_weight))
    out_z = gather_all_to_all(out_weight, "z", z_size).reshape(-1, out_shape[1])
    qkv_t = gather_pair(qkv_t, "xh").reshape(-1, units)
    projection_t = gather_pair(qkv_t, "grp").reshape(-1, units)

    group_width = qkv_weight.shape[1]
    heads_here = group_width // HD
    samples = rewards.shape[0]
    seq_len = latents.shape[1]
    block_rows = min(512, seq_len)
    advantage = advantages(rewards, group_ids)
    loss_value, coef = policy_terms(advantage, log_ratio)
    my_index = lax.axis_index(SAMPLE_AXES)
    chooser = (jnp.arange(samples, dtype=jnp.int32) == my_index).astype(jnp.float32)
    my_coef = jnp.sum(coef * chooser[None, :], 1)
    step_size = 1.0 / TSTEPS
    state = latents[0]
    attn_list = []
    score_list = []
    plan = jnp.arange(TSTEPS, dtype=jnp.int32)
    for section in range(2):
        index_now = time_index[0] + section
        time_now = 1.0 - index_now.astype(jnp.float32) / TSTEPS
        picker = (plan == index_now).astype(jnp.float32)
        modulate = jnp.sum(picker[:, None, None] * ada_table, 0)
        if section == 0:
            blocks = first_blocks
        else:
            blocks = gather_all_to_all(state.astype(jnp.bfloat16), FEATURE_AXES, seq_size)
        whole = jnp.transpose(blocks, (1, 0, 2)).reshape(seq_len, -1).astype(jnp.float32)
        centre = jnp.mean(whole, -1, keepdims=True)
        spread = jnp.mean((whole - centre) ** 2, -1, keepdims=True)
        normed = (
            (whole - centre) * lax.rsqrt(spread + NORM_EPS) * (1.0 + modulate[0][None, :])
            + modulate[1][None, :]
        ).astype(jnp.bfloat16)
        proj_rows = jnp.dot(normed, projection_t, preferred_element_type=jnp.float32).astype(
            jnp.bfloat16
        )
        proj_rows = proj_rows.reshape(seq_len, 3, heads_here, HD)
        key_rows = proj_rows[:, 1]
        value_rows = proj_rows[:, 2]
        query_rows = proj_rows[0:block_rows, 0]
        logits = jnp.einsum(
            "qhe,khe->hqk", query_rows, key_rows, preferred_element_type=jnp.float32
        ) * HD ** (-0.5)
        logits = logits - jnp.max(logits, -1, keepdims=True)
        weights = jnp.exp(logits)
        probs = (weights / jnp.sum(weights, -1, keepdims=True)).astype(jnp.bfloat16)
        attn_blocks = jnp.einsum(
            "hqk,khe->qhe", probs, value_rows, preferred_element_type=jnp.float32
        ).astype(jnp.bfloat16)
        attn = attn_blocks.reshape(seq_len, group_width)
        if section == 0:
            out_z, attn = lax.optimization_barrier((out_z, attn))
            out_rows = gather_pair(out_z, "xh").reshape(-1, out_shape[1])
            out_rows = gather_pair(out_rows, "grp").reshape(-1, out_shape[1])
        attn_parts = gather_all_to_all(attn, FEATURE_AXES, seq_size)
        attn_all = jnp.transpose(attn_parts, (1, 0, 2)).reshape(seq_len, -1)
        velocity = jnp.dot(attn_all, out_rows, preferred_element_type=jnp.float32)
        noise_level = SDE_NOISE * SDE_NOISE * time_now / (1.0 - time_now)
        std_dev = jnp.sqrt(noise_level * step_size)
        drift = velocity + noise_level / (2.0 * time_now) * (state + (1.0 - time_now) * velocity)
        mean_next = state - step_size * drift
        noise_now = step_noise[section, 0].astype(jnp.float32)
        state = mean_next + std_dev * noise_now
        factor = (
            my_coef[section]
            * -step_size
            * (1.0 + noise_level * (1.0 - time_now) / (2.0 * time_now))
            / std_dev
        )
        score_list.append((factor * noise_now).astype(jnp.bfloat16))
        attn_list.append(attn_all)
    attn_both = jnp.stack(attn_list, 0)
    score_both = jnp.stack(score_list, 0)
    rows = attn_both.shape[2]
    attn_halves = attn_both.reshape(attn_both.shape[0], attn_both.shape[1], 2, rows // 2)
    part = lax.dot_general(
        attn_halves, score_both, (((0, 1), (0, 1)), ((), ())), preferred_element_type=jnp.float32
    )
    part = reduce_pair(part, "grp")
    part = part.reshape(2, rows // 4, -1)
    part = reduce_pair(part, "xh")
    part = part.reshape(z_size, rows // (4 * z_size), -1)
    part = lax.all_to_all(part.astype(jnp.bfloat16), "z", 0, 0, tiled=True)
    out_grad = jnp.sum(part.astype(jnp.float32), 0)
    return (state[None], loss_value, out_grad)


def solution(mesh):
    grp, dp, seq = (mesh.shape[a] for a in ("grp", "dp", "seq"))
    xh, xl = 2, 2
    z_size, y_size = dp // xh, seq // xl
    fine = Mesh(
        mesh.devices.reshape(grp, xh, z_size, y_size, xl), ("grp", "xh", "z", "y", "xl")
    )
    samples = SAMPLE_AXES
    features = FEATURE_AXES

    def body(*args):
        return on_device(*args, z_size=z_size, seq_size=seq)

    return jax.shard_map(
        body,
        mesh=fine,
        in_specs=(
            P(samples, None, features),
            P(None, samples, None, features),
            P(),
            P(None, features, samples),
            P(samples, features),
            P(),
            P(),
            P(samples),
            P(),
        ),
        out_specs=(P(samples, None, features), P(), P(samples, features)),
        check_vma=False,
    )
```

```python
import jax
import jax.numpy as jnp
from jax import lax
from jax.sharding import Mesh
from jax.sharding import PartitionSpec as P

HD = 64
TSTEPS = 10
GSIZE = 8


SDE_NOISE = 0.7
CLIP_RANGE = 0.2
REWARD_FLOOR = 0.75
NORM_EPS = 1e-06

SAMPLE_AXES = ("grp", "xh", "z")
FEATURE_AXES = ("y", "xl")


def advantages(rewards, group_ids):
    same_group = (group_ids[:, None] == group_ids[None, :]).astype(jnp.float32)
    centre = jnp.sum(same_group * rewards[None, :], 1) / GSIZE
    spread = jnp.sum(same_group * (rewards[None, :] - centre[:, None]) ** 2, 1) / GSIZE
    return (rewards - centre) / jnp.maximum(jnp.sqrt(spread), REWARD_FLOOR)


def policy_terms(advantage, log_ratio):
    ratios = jnp.exp(log_ratio)
    plain = ratios * advantage[None, :]
    bounded = jnp.clip(ratios, 1.0 - CLIP_RANGE, 1.0 + CLIP_RANGE) * advantage[None, :]
    count = 2.0 * advantage.shape[0]
    loss_value = -jnp.sum(jnp.minimum(plain, bounded)) / count
    coef = jnp.where(plain <= bounded, -plain / count, jnp.float32(0.0))
    return (loss_value, coef)


def gather_all_to_all(x, axis_name, size):
    spread = jnp.broadcast_to(x[None], (size,) + x.shape)
    return lax.all_to_all(spread, axis_name, 0, 0, tiled=True)


def gather_pair(x, axis_name):
    other = lax.ppermute(x, axis_name, [(0, 1), (1, 0)])
    first = lax.axis_index(axis_name) == 0
    return jnp.where(first, jnp.stack([x, other]), jnp.stack([other, x]))


def reduce_pair(x, axis_name):
    me = lax.axis_index(axis_name)
    keep = lax.dynamic_index_in_dim(x, me, 0, keepdims=False)
    send = lax.dynamic_index_in_dim(x, 1 - me, 0, keepdims=False)
    sent = lax.ppermute(send.astype(jnp.bfloat16), axis_name, [(0, 1), (1, 0)])
    return keep + sent.astype(keep.dtype)


def on_device(
    latents,
    step_noise,
    ada_table,
    qkv_weight,
    out_weight,
    rewards,
    group_ids,
    time_index,
    log_ratio,
    z_size,
    seq_size,
):
    units = qkv_weight.shape[0] * qkv_weight.shape[1]
    qkv_t = jnp.transpose(qkv_weight, (2, 0, 1)).reshape(qkv_weight.shape[2], units)
    qkv_t = lax.all_gather(qkv_t, "z", axis=0, tiled=True)
    qkv_t = gather_pair(qkv_t, "xh").reshape(-1, units)
    projection_t = gather_pair(qkv_t, "grp").reshape(-1, units)
    first_blocks = gather_all_to_all(latents[0].astype(jnp.bfloat16), FEATURE_AXES, seq_size)
    first_blocks, out_weight = lax.optimization_barrier((first_blocks, out_weight))
    out_rows = gather_all_to_all(out_weight, "z", z_size).reshape(-1, out_weight.shape[1])
    out_rows = gather_pair(out_rows, "xh").reshape(-1, out_weight.shape[1])
    out_rows = gather_pair(out_rows, "grp").reshape(-1, out_weight.shape[1])

    group_width = qkv_weight.shape[1]
    heads_here = group_width // HD
    samples = rewards.shape[0]
    seq_len = latents.shape[1]
    block_rows = min(512, seq_len)
    advantage = advantages(rewards, group_ids)
    loss_value, coef = policy_terms(advantage, log_ratio)
    my_index = lax.axis_index(SAMPLE_AXES)
    chooser = (jnp.arange(samples, dtype=jnp.int32) == my_index).astype(jnp.float32)
    my_coef = jnp.sum(coef * chooser[None, :], 1)
    step_size = 1.0 / TSTEPS
    state = latents[0]
    attn_list = []
    score_list = []
    plan = jnp.arange(TSTEPS, dtype=jnp.int32)
    for section in range(2):
        index_now = time_index[0] + section
        time_now = 1.0 - index_now.astype(jnp.float32) / TSTEPS
        picker = (plan == index_now).astype(jnp.float32)
        modulate = jnp.sum(picker[:, None, None] * ada_table, 0)
        if section == 0:
            blocks = first_blocks
        else:
            blocks = gather_all_to_all(state.astype(jnp.bfloat16), FEATURE_AXES, seq_size)
        whole = jnp.transpose(blocks, (1, 0, 2)).reshape(seq_len, -1).astype(jnp.float32)
        centre = jnp.mean(whole, -1, keepdims=True)
        spread = jnp.mean((whole - centre) ** 2, -1, keepdims=True)
        normed = (
            (whole - centre) * lax.rsqrt(spread + NORM_EPS) * (1.0 + modulate[0][None, :])
            + modulate[1][None, :]
        ).astype(jnp.bfloat16)
        proj_rows = jnp.dot(normed, projection_t, preferred_element_type=jnp.float32).astype(
            jnp.bfloat16
        )
        proj_rows = proj_rows.reshape(seq_len, 3, heads_here, HD)
        key_rows = proj_rows[:, 1]
        value_rows = proj_rows[:, 2]
        query_rows = proj_rows[0:block_rows, 0]
        logits = jnp.einsum(
            "qhe,khe->hqk", query_rows, key_rows, preferred_element_type=jnp.float32
        ) * HD ** (-0.5)
        logits = logits - jnp.max(logits, -1, keepdims=True)
        weights = jnp.exp(logits)
        probs = (weights / jnp.sum(weights, -1, keepdims=True)).astype(jnp.bfloat16)
        attn_blocks = jnp.einsum(
            "hqk,khe->qhe", probs, value_rows, preferred_element_type=jnp.float32
        ).astype(jnp.bfloat16)
        attn = attn_blocks.reshape(seq_len, group_width)
        attn_parts = gather_all_to_all(attn, FEATURE_AXES, seq_size)
        attn_all = jnp.transpose(attn_parts, (1, 0, 2)).reshape(seq_len, -1)
        velocity = jnp.dot(attn_all, out_rows, preferred_element_type=jnp.float32)
        noise_level = SDE_NOISE * SDE_NOISE * time_now / (1.0 - time_now)
        std_dev = jnp.sqrt(noise_level * step_size)
        drift = velocity + noise_level / (2.0 * time_now) * (state + (1.0 - time_now) * velocity)
        mean_next = state - step_size * drift
        noise_now = step_noise[section, 0].astype(jnp.float32)
        state = mean_next + std_dev * noise_now
        factor = (
            my_coef[section]
            * -step_size
            * (1.0 + noise_level * (1.0 - time_now) / (2.0 * time_now))
            / std_dev
        )
        score_list.append((factor * noise_now).astype(jnp.bfloat16))
        attn_list.append(attn_all)
    attn_both = jnp.stack(attn_list, 0)
    score_both = jnp.stack(score_list, 0)
    rows = attn_both.shape[2]
    attn_halves = attn_both.reshape(attn_both.shape[0], attn_both.shape[1], 2, rows // 2)
    part = lax.dot_general(
        attn_halves, score_both, (((0, 1), (0, 1)), ((), ())), preferred_element_type=jnp.float32
    )
    part = reduce_pair(part, "grp")
    part = part.reshape(2, rows // 4, -1)
    part = reduce_pair(part, "xh")
    part = part.reshape(z_size, rows // (4 * z_size), -1)
    part = lax.all_to_all(part.astype(jnp.bfloat16), "z", 0, 0, tiled=True)
    out_grad = jnp.sum(part.astype(jnp.float32), 0)
    return (state[None], loss_value, out_grad)


def solution(mesh):
    grp, dp, seq = (mesh.shape[a] for a in ("grp", "dp", "seq"))
    xh, xl = 2, 2
    z_size, y_size = dp // xh, seq // xl
    fine = Mesh(
        mesh.devices.reshape(grp, xh, z_size, y_size, xl), ("grp", "xh", "z", "y", "xl")
    )
    samples = SAMPLE_AXES
    features = FEATURE_AXES

    def body(*args):
        return on_device(*args, z_size=z_size, seq_size=seq)

    return jax.shard_map(
        body,
        mesh=fine,
        in_specs=(
            P(samples, None, features),
            P(None, samples, None, features),
            P(),
            P(None, features, samples),
            P(samples, features),
            P(),
            P(),
            P(samples),
            P(),
        ),
        out_specs=(P(samples, None, features), P(), P(samples, features)),
        check_vma=False,
    )
```

```python
import jax
import jax.numpy as jnp
from jax import lax
from jax.sharding import Mesh
from jax.sharding import PartitionSpec as P

HD = 64
TSTEPS = 10
GSIZE = 8


SDE_NOISE = 0.7
CLIP_RANGE = 0.2
REWARD_FLOOR = 0.75
NORM_EPS = 1e-06

SAMPLE_AXES = ("grp", "xh", "z")
FEATURE_AXES = ("y", "xl")


def advantages(rewards, group_ids):
    same_group = (group_ids[:, None] == group_ids[None, :]).astype(jnp.float32)
    centre = jnp.sum(same_group * rewards[None, :], 1) / GSIZE
    spread = jnp.sum(same_group * (rewards[None, :] - centre[:, None]) ** 2, 1) / GSIZE
    return (rewards - centre) / jnp.maximum(jnp.sqrt(spread), REWARD_FLOOR)


def policy_terms(advantage, log_ratio):
    ratios = jnp.exp(log_ratio)
    plain = ratios * advantage[None, :]
    bounded = jnp.clip(ratios, 1.0 - CLIP_RANGE, 1.0 + CLIP_RANGE) * advantage[None, :]
    count = 2.0 * advantage.shape[0]
    loss_value = -jnp.sum(jnp.minimum(plain, bounded)) / count
    coef = jnp.where(plain <= bounded, -plain / count, jnp.float32(0.0))
    return (loss_value, coef)


def gather_all_to_all(x, axis_name, size):
    spread = jnp.broadcast_to(x[None], (size,) + x.shape)
    return lax.all_to_all(spread, axis_name, 0, 0, tiled=True)


def gather_pair(x, axis_name):
    other = lax.ppermute(x, axis_name, [(0, 1), (1, 0)])
    first = lax.axis_index(axis_name) == 0
    return jnp.where(first, jnp.stack([x, other]), jnp.stack([other, x]))


def reduce_pair(x, axis_name):
    me = lax.axis_index(axis_name)
    keep = lax.dynamic_index_in_dim(x, me, 0, keepdims=False)
    send = lax.dynamic_index_in_dim(x, 1 - me, 0, keepdims=False)
    sent = lax.ppermute(send.astype(jnp.bfloat16), axis_name, [(0, 1), (1, 0)])
    return keep + sent.astype(keep.dtype)


def on_device(
    latents,
    step_noise,
    ada_table,
    qkv_weight,
    out_weight,
    rewards,
    group_ids,
    time_index,
    log_ratio,
    z_size,
    seq_size,
    samples_total,
):
    units = qkv_weight.shape[0] * qkv_weight.shape[1]
    qkv_t = jnp.transpose(qkv_weight, (2, 0, 1)).reshape(qkv_weight.shape[2], units)
    qkv_t = lax.all_gather(qkv_t, "z", axis=0, tiled=True)
    qkv_t = gather_pair(qkv_t, "xh").reshape(-1, units)
    projection_t = gather_pair(qkv_t, "grp").reshape(-1, units)
    first_blocks = gather_all_to_all(latents[0].astype(jnp.bfloat16), FEATURE_AXES, seq_size)
    noise_parts = gather_all_to_all(step_noise[:, 0], FEATURE_AXES, seq_size)
    noise_full = jnp.transpose(noise_parts, (1, 2, 0, 3)).reshape(
        step_noise.shape[0], latents.shape[1], -1
    )
    first_blocks, out_weight = lax.optimization_barrier((first_blocks, out_weight))
    out_rows = gather_all_to_all(out_weight, "z", z_size).reshape(-1, out_weight.shape[1])
    out_rows = gather_pair(out_rows, "xh").reshape(-1, out_weight.shape[1])
    out_rows = gather_pair(out_rows, "grp").reshape(-1, out_weight.shape[1])

    group_width = qkv_weight.shape[1]
    heads_here = group_width // HD
    samples = rewards.shape[0]
    seq_len = latents.shape[1]
    block_rows = min(512, seq_len)
    advantage = advantages(rewards, group_ids)
    loss_value, coef = policy_terms(advantage, log_ratio)
    my_index = lax.axis_index(SAMPLE_AXES)
    chooser = (jnp.arange(samples, dtype=jnp.int32) == my_index).astype(jnp.float32)
    my_coef = jnp.sum(coef * chooser[None, :], 1)
    step_size = 1.0 / TSTEPS
    state = latents[0]
    attn_list = []
    score_list = []
    plan = jnp.arange(TSTEPS, dtype=jnp.int32)
    for section in range(2):
        index_now = time_index[0] + section
        time_now = 1.0 - index_now.astype(jnp.float32) / TSTEPS
        picker = (plan == index_now).astype(jnp.float32)
        modulate = jnp.sum(picker[:, None, None] * ada_table, 0)
        if section == 0:
            blocks = first_blocks
        else:
            blocks = gather_all_to_all(state.astype(jnp.bfloat16), FEATURE_AXES, seq_size)
        whole = jnp.transpose(blocks, (1, 0, 2)).reshape(seq_len, -1).astype(jnp.float32)
        centre = jnp.mean(whole, -1, keepdims=True)
        spread = jnp.mean((whole - centre) ** 2, -1, keepdims=True)
        normed = (
            (whole - centre) * lax.rsqrt(spread + NORM_EPS) * (1.0 + modulate[0][None, :])
            + modulate[1][None, :]
        ).astype(jnp.bfloat16)
        proj_rows = jnp.dot(normed, projection_t, preferred_element_type=jnp.float32).astype(
            jnp.bfloat16
        )
        proj_rows = proj_rows.reshape(seq_len, 3, heads_here, HD)
        key_rows = proj_rows[:, 1]
        value_rows = proj_rows[:, 2]
        query_rows = proj_rows[0:block_rows, 0]
        logits = jnp.einsum(
            "qhe,khe->hqk", query_rows, key_rows, preferred_element_type=jnp.float32
        ) * HD ** (-0.5)
        logits = logits - jnp.max(logits, -1, keepdims=True)
        weights = jnp.exp(logits)
        probs = (weights / jnp.sum(weights, -1, keepdims=True)).astype(jnp.bfloat16)
        attn_blocks = jnp.einsum(
            "hqk,khe->qhe", probs, value_rows, preferred_element_type=jnp.float32
        ).astype(jnp.bfloat16)
        attn = attn_blocks.reshape(seq_len, group_width)
        attn_parts = gather_all_to_all(attn, FEATURE_AXES, seq_size)
        attn_all = jnp.transpose(attn_parts, (1, 0, 2)).reshape(seq_len, -1)
        velocity = jnp.dot(attn_all, out_rows, preferred_element_type=jnp.float32)
        noise_level = SDE_NOISE * SDE_NOISE * time_now / (1.0 - time_now)
        std_dev = jnp.sqrt(noise_level * step_size)
        drift = velocity + noise_level / (2.0 * time_now) * (state + (1.0 - time_now) * velocity)
        mean_next = state - step_size * drift
        noise_now = step_noise[section, 0].astype(jnp.float32)
        state = mean_next + std_dev * noise_now
        factor = (
            my_coef[section]
            * -step_size
            * (1.0 + noise_level * (1.0 - time_now) / (2.0 * time_now))
            / std_dev
        )
        score_list.append((factor * noise_full[section].astype(jnp.float32)).astype(jnp.bfloat16))
        attn_list.append(attn)
    attn_both = jnp.stack(attn_list, 0)
    score_both = jnp.stack(score_list, 0)
    rows_here = lax.dot_general(
        attn_both, score_both, (((0, 1), (0, 1)), ((), ())), preferred_element_type=jnp.float32
    )
    out_shape = out_weight.shape
    row_blocks = rows_here.shape[0] // out_shape[0]
    feature_block = out_shape[1]
    part = rows_here.reshape(row_blocks, out_shape[0], 2, 2, 2, feature_block)
    part = jnp.transpose(part, (2, 3, 4, 0, 1, 5))
    part = reduce_pair(part, "grp")
    part = reduce_pair(part, "xh")
    part = part.reshape(z_size, out_shape[0], feature_block)
    part = lax.all_to_all(part.astype(jnp.bfloat16), "z", 0, 0, tiled=True)
    summed = jnp.sum(part.astype(jnp.float32), 0)
    owners = samples_total
    pairs = [
        (q * seq_size + f, ((f * row_blocks) + q % row_blocks) * seq_size + q // row_blocks)
        for q in range(owners)
        for f in range(seq_size)
    ]
    out_grad = lax.ppermute(summed, SAMPLE_AXES + FEATURE_AXES, pairs)
    return (state[None], loss_value, out_grad)


def solution(mesh):
    grp, dp, seq = (mesh.shape[a] for a in ("grp", "dp", "seq"))
    xh, xl = 2, 2
    z_size, y_size = dp // xh, seq // xl
    fine = Mesh(
        mesh.devices.reshape(grp, xh, z_size, y_size, xl), ("grp", "xh", "z", "y", "xl")
    )
    samples = SAMPLE_AXES
    features = FEATURE_AXES

    def body(*args):
        return on_device(*args, z_size=z_size, seq_size=seq, samples_total=grp * dp)

    return jax.shard_map(
        body,
        mesh=fine,
        in_specs=(
            P(samples, None, features),
            P(None, samples, None, features),
            P(),
            P(None, features, samples),
            P(samples, features),
            P(),
            P(),
            P(samples),
            P(),
        ),
        out_specs=(P(samples, None, features), P(), P(samples, features)),
        check_vma=False,
    )
```

```python
import jax
import jax.numpy as jnp
from jax import lax
from jax.sharding import Mesh
from jax.sharding import PartitionSpec as P

HD = 64
TSTEPS = 10
GSIZE = 8


SDE_NOISE = 0.7
CLIP_RANGE = 0.2
REWARD_FLOOR = 0.75
NORM_EPS = 1e-06

SAMPLE_AXES = ("grp", "xh", "z")
FEATURE_AXES = ("y", "xl")


def advantages(rewards, group_ids):
    same_group = (group_ids[:, None] == group_ids[None, :]).astype(jnp.float32)
    centre = jnp.sum(same_group * rewards[None, :], 1) / GSIZE
    spread = jnp.sum(same_group * (rewards[None, :] - centre[:, None]) ** 2, 1) / GSIZE
    return (rewards - centre) / jnp.maximum(jnp.sqrt(spread), REWARD_FLOOR)


def policy_terms(advantage, log_ratio):
    ratios = jnp.exp(log_ratio)
    plain = ratios * advantage[None, :]
    bounded = jnp.clip(ratios, 1.0 - CLIP_RANGE, 1.0 + CLIP_RANGE) * advantage[None, :]
    count = 2.0 * advantage.shape[0]
    loss_value = -jnp.sum(jnp.minimum(plain, bounded)) / count
    coef = jnp.where(plain <= bounded, -plain / count, jnp.float32(0.0))
    return (loss_value, coef)


def gather_all_to_all(x, axis_name, size):
    spread = jnp.broadcast_to(x[None], (size,) + x.shape)
    return lax.all_to_all(spread, axis_name, 0, 0, tiled=True)


def gather_pair(x, axis_name):
    other = lax.ppermute(x, axis_name, [(0, 1), (1, 0)])
    first = lax.axis_index(axis_name) == 0
    return jnp.where(first, jnp.stack([x, other]), jnp.stack([other, x]))


def reduce_pair(x, axis_name):
    me = lax.axis_index(axis_name)
    keep = lax.dynamic_index_in_dim(x, me, 0, keepdims=False)
    send = lax.dynamic_index_in_dim(x, 1 - me, 0, keepdims=False)
    sent = lax.ppermute(send.astype(jnp.bfloat16), axis_name, [(0, 1), (1, 0)])
    return keep + sent.astype(keep.dtype)


def on_device(
    latents,
    step_noise,
    ada_table,
    qkv_weight,
    out_weight,
    rewards,
    group_ids,
    time_index,
    log_ratio,
    z_size,
    seq_size,
):
    units = qkv_weight.shape[0] * qkv_weight.shape[1]
    qkv_t = jnp.transpose(qkv_weight, (2, 0, 1)).reshape(qkv_weight.shape[2], units)
    qkv_t = lax.all_gather(qkv_t, "z", axis=0, tiled=True)
    swap = [(0, 1), (1, 0)]
    me_g, me_x = lax.axis_index("grp"), lax.axis_index("xh")
    from_x = lax.ppermute(qkv_t, "xh", swap)
    from_g = lax.ppermute(qkv_t, "grp", swap)
    from_gx = lax.ppermute(from_x, "grp", swap)
    block_rows = qkv_t.shape[0]
    weight_blocks = [
        ((me_g * 2 + me_x) * block_rows, qkv_t),
        ((me_g * 2 + 1 - me_x) * block_rows, from_x),
        (((1 - me_g) * 2 + me_x) * block_rows, from_g),
        (((1 - me_g) * 2 + 1 - me_x) * block_rows, from_gx),
    ]
    first_blocks = gather_all_to_all(latents[0].astype(jnp.bfloat16), FEATURE_AXES, seq_size)
    first_blocks, out_weight = lax.optimization_barrier((first_blocks, out_weight))
    out_rows = gather_all_to_all(out_weight, "z", z_size).reshape(-1, out_weight.shape[1])
    out_rows = gather_pair(out_rows, "xh").reshape(-1, out_weight.shape[1])
    out_rows = gather_pair(out_rows, "grp").reshape(-1, out_weight.shape[1])

    group_width = qkv_weight.shape[1]
    heads_here = group_width // HD
    samples = rewards.shape[0]
    seq_len = latents.shape[1]
    query_count = min(512, seq_len)
    advantage = advantages(rewards, group_ids)
    loss_value, coef = policy_terms(advantage, log_ratio)
    my_index = lax.axis_index(SAMPLE_AXES)
    chooser = (jnp.arange(samples, dtype=jnp.int32) == my_index).astype(jnp.float32)
    my_coef = jnp.sum(coef * chooser[None, :], 1)
    step_size = 1.0 / TSTEPS
    state = latents[0]
    attn_list = []
    score_list = []
    plan = jnp.arange(TSTEPS, dtype=jnp.int32)
    for section in range(2):
        index_now = time_index[0] + section
        time_now = 1.0 - index_now.astype(jnp.float32) / TSTEPS
        picker = (plan == index_now).astype(jnp.float32)
        modulate = jnp.sum(picker[:, None, None] * ada_table, 0)
        if section == 0:
            blocks = first_blocks
        else:
            blocks = gather_all_to_all(state.astype(jnp.bfloat16), FEATURE_AXES, seq_size)
        whole = jnp.transpose(blocks, (1, 0, 2)).reshape(seq_len, -1).astype(jnp.float32)
        centre = jnp.mean(whole, -1, keepdims=True)
        spread = jnp.mean((whole - centre) ** 2, -1, keepdims=True)
        normed = (
            (whole - centre) * lax.rsqrt(spread + NORM_EPS) * (1.0 + modulate[0][None, :])
            + modulate[1][None, :]
        ).astype(jnp.bfloat16)
        proj_sum = None
        for offset, block in weight_blocks:
            columns = lax.dynamic_slice_in_dim(normed, offset, block.shape[0], axis=1)
            term = jnp.dot(columns, block, preferred_element_type=jnp.float32)
            proj_sum = term if proj_sum is None else proj_sum + term
        proj_rows = proj_sum.astype(jnp.bfloat16)
        proj_rows = proj_rows.reshape(seq_len, 3, heads_here, HD)
        key_rows = proj_rows[:, 1]
        value_rows = proj_rows[:, 2]
        query_rows = proj_rows[0:query_count, 0]
        logits = jnp.einsum(
            "qhe,khe->hqk", query_rows, key_rows, preferred_element_type=jnp.float32
        ) * HD ** (-0.5)
        logits = logits - jnp.max(logits, -1, keepdims=True)
        weights = jnp.exp(logits)
        probs = (weights / jnp.sum(weights, -1, keepdims=True)).astype(jnp.bfloat16)
        attn_blocks = jnp.einsum(
            "hqk,khe->qhe", probs, value_rows, preferred_element_type=jnp.float32
        ).astype(jnp.bfloat16)
        attn = attn_blocks.reshape(seq_len, group_width)
        attn_parts = gather_all_to_all(attn, FEATURE_AXES, seq_size)
        attn_all = jnp.transpose(attn_parts, (1, 0, 2)).reshape(seq_len, -1)
        velocity = jnp.dot(attn_all, out_rows, preferred_element_type=jnp.float32)
        noise_level = SDE_NOISE * SDE_NOISE * time_now / (1.0 - time_now)
        std_dev = jnp.sqrt(noise_level * step_size)
        drift = velocity + noise_level / (2.0 * time_now) * (state + (1.0 - time_now) * velocity)
        mean_next = state - step_size * drift
        noise_now = step_noise[section, 0].astype(jnp.float32)
        state = mean_next + std_dev * noise_now
        factor = (
            my_coef[section]
            * -step_size
            * (1.0 + noise_level * (1.0 - time_now) / (2.0 * time_now))
            / std_dev
        )
        score_list.append((factor * noise_now).astype(jnp.bfloat16))
        attn_list.append(attn_all)
    attn_both = jnp.stack(attn_list, 0)
    score_both = jnp.stack(score_list, 0)
    rows = attn_both.shape[2]
    attn_halves = attn_both.reshape(attn_both.shape[0], attn_both.shape[1], 2, rows // 2)
    part = lax.dot_general(
        attn_halves, score_both, (((0, 1), (0, 1)), ((), ())), preferred_element_type=jnp.float32
    )
    part = reduce_pair(part, "grp")
    part = part.reshape(2, rows // 4, -1)
    part = reduce_pair(part, "xh")
    part = part.reshape(z_size, rows // (4 * z_size), -1)
    part = lax.all_to_all(part.astype(jnp.bfloat16), "z", 0, 0, tiled=True)
    out_grad = jnp.sum(part.astype(jnp.float32), 0)
    return (state[None], loss_value, out_grad)


def solution(mesh):
    grp, dp, seq = (mesh.shape[a] for a in ("grp", "dp", "seq"))
    xh, xl = 2, 2
    z_size, y_size = dp // xh, seq // xl
    fine = Mesh(
        mesh.devices.reshape(grp, xh, z_size, y_size, xl), ("grp", "xh", "z", "y", "xl")
    )
    samples = SAMPLE_AXES
    features = FEATURE_AXES

    def body(*args):
        return on_device(*args, z_size=z_size, seq_size=seq)

    return jax.shard_map(
        body,
        mesh=fine,
        in_specs=(
            P(samples, None, features),
            P(None, samples, None, features),
            P(),
            P(None, features, samples),
            P(samples, features),
            P(),
            P(),
            P(samples),
            P(),
        ),
        out_specs=(P(samples, None, features), P(), P(samples, features)),
        check_vma=False,
    )
```

```python
import jax
import jax.numpy as jnp
from jax import lax
from jax.sharding import Mesh
from jax.sharding import PartitionSpec as P

HD = 64
TSTEPS = 10
GSIZE = 8


SDE_NOISE = 0.7
CLIP_RANGE = 0.2
REWARD_FLOOR = 0.75
NORM_EPS = 1e-06

SAMPLE_AXES = ("grp", "xh", "z")
FEATURE_AXES = ("y", "xl")


def advantages(rewards, group_ids):
    same_group = (group_ids[:, None] == group_ids[None, :]).astype(jnp.float32)
    centre = jnp.sum(same_group * rewards[None, :], 1) / GSIZE
    spread = jnp.sum(same_group * (rewards[None, :] - centre[:, None]) ** 2, 1) / GSIZE
    return (rewards - centre) / jnp.maximum(jnp.sqrt(spread), REWARD_FLOOR)


def policy_terms(advantage, log_ratio):
    ratios = jnp.exp(log_ratio)
    plain = ratios * advantage[None, :]
    bounded = jnp.clip(ratios, 1.0 - CLIP_RANGE, 1.0 + CLIP_RANGE) * advantage[None, :]
    count = 2.0 * advantage.shape[0]
    loss_value = -jnp.sum(jnp.minimum(plain, bounded)) / count
    coef = jnp.where(plain <= bounded, -plain / count, jnp.float32(0.0))
    return (loss_value, coef)


def gather_all_to_all(x, axis_name, size):
    spread = jnp.broadcast_to(x[None], (size,) + x.shape)
    return lax.all_to_all(spread, axis_name, 0, 0, tiled=True)


def gather_pair(x, axis_name):
    other = lax.ppermute(x, axis_name, [(0, 1), (1, 0)])
    first = lax.axis_index(axis_name) == 0
    return jnp.where(first, jnp.stack([x, other]), jnp.stack([other, x]))


def reduce_pair(x, axis_name):
    me = lax.axis_index(axis_name)
    keep = lax.dynamic_index_in_dim(x, me, 0, keepdims=False)
    send = lax.dynamic_index_in_dim(x, 1 - me, 0, keepdims=False)
    sent = lax.ppermute(send.astype(jnp.bfloat16), axis_name, [(0, 1), (1, 0)])
    return keep + sent.astype(keep.dtype)


def on_device(
    latents,
    step_noise,
    ada_table,
    qkv_weight,
    out_weight,
    rewards,
    group_ids,
    time_index,
    log_ratio,
    z_size,
    seq_size,
):
    units = qkv_weight.shape[0] * qkv_weight.shape[1]
    qkv_t = jnp.transpose(qkv_weight, (2, 0, 1)).reshape(qkv_weight.shape[2], units)
    qkv_t = lax.all_gather(qkv_t, "z", axis=0, tiled=True)
    first_blocks = gather_all_to_all(latents[0].astype(jnp.bfloat16), FEATURE_AXES, seq_size)
    first_blocks, out_weight, qkv_t = lax.optimization_barrier((first_blocks, out_weight, qkv_t))
    out_z = gather_all_to_all(out_weight, "z", z_size)
    swap = [(0, 1), (1, 0)]
    me_g, me_x = lax.axis_index("grp"), lax.axis_index("xh")
    from_x = lax.ppermute(qkv_t, "xh", swap)
    from_g = lax.ppermute(qkv_t, "grp", swap)
    from_gx = lax.ppermute(from_x, "grp", swap)
    block_rows = qkv_t.shape[0]
    weight_blocks = [
        ((me_g * 2 + me_x) * block_rows, qkv_t),
        ((me_g * 2 + 1 - me_x) * block_rows, from_x),
        (((1 - me_g) * 2 + me_x) * block_rows, from_g),
        (((1 - me_g) * 2 + 1 - me_x) * block_rows, from_gx),
    ]
    out_rows = out_z.reshape(-1, out_weight.shape[1])
    out_rows = gather_pair(out_rows, "xh").reshape(-1, out_weight.shape[1])
    out_rows = gather_pair(out_rows, "grp").reshape(-1, out_weight.shape[1])

    group_width = qkv_weight.shape[1]
    heads_here = group_width // HD
    samples = rewards.shape[0]
    seq_len = latents.shape[1]
    query_count = min(512, seq_len)
    advantage = advantages(rewards, group_ids)
    loss_value, coef = policy_terms(advantage, log_ratio)
    my_index = lax.axis_index(SAMPLE_AXES)
    chooser = (jnp.arange(samples, dtype=jnp.int32) == my_index).astype(jnp.float32)
    my_coef = jnp.sum(coef * chooser[None, :], 1)
    step_size = 1.0 / TSTEPS
    state = latents[0]
    attn_list = []
    score_list = []
    plan = jnp.arange(TSTEPS, dtype=jnp.int32)
    for section in range(2):
        index_now = time_index[0] + section
        time_now = 1.0 - index_now.astype(jnp.float32) / TSTEPS
        picker = (plan == index_now).astype(jnp.float32)
        modulate = jnp.sum(picker[:, None, None] * ada_table, 0)
        if section == 0:
            blocks = first_blocks
        else:
            blocks = gather_all_to_all(state.astype(jnp.bfloat16), FEATURE_AXES, seq_size)
        whole = jnp.transpose(blocks, (1, 0, 2)).reshape(seq_len, -1).astype(jnp.float32)
        centre = jnp.mean(whole, -1, keepdims=True)
        spread = jnp.mean((whole - centre) ** 2, -1, keepdims=True)
        normed = (
            (whole - centre) * lax.rsqrt(spread + NORM_EPS) * (1.0 + modulate[0][None, :])
            + modulate[1][None, :]
        ).astype(jnp.bfloat16)
        proj_sum = None
        for offset, block in weight_blocks:
            columns = lax.dynamic_slice_in_dim(normed, offset, block.shape[0], axis=1)
            term = jnp.dot(columns, block, preferred_element_type=jnp.float32)
            proj_sum = term if proj_sum is None else proj_sum + term
        proj_rows = proj_sum.astype(jnp.bfloat16)
        proj_rows = proj_rows.reshape(seq_len, 3, heads_here, HD)
        key_rows = proj_rows[:, 1]
        value_rows = proj_rows[:, 2]
        query_rows = proj_rows[0:query_count, 0]
        logits = jnp.einsum(
            "qhe,khe->hqk", query_rows, key_rows, preferred_element_type=jnp.float32
        ) * HD ** (-0.5)
        logits = logits - jnp.max(logits, -1, keepdims=True)
        weights = jnp.exp(logits)
        probs = (weights / jnp.sum(weights, -1, keepdims=True)).astype(jnp.bfloat16)
        attn_blocks = jnp.einsum(
            "hqk,khe->qhe", probs, value_rows, preferred_element_type=jnp.float32
        ).astype(jnp.bfloat16)
        attn = attn_blocks.reshape(seq_len, group_width)
        attn_parts = gather_all_to_all(attn, FEATURE_AXES, seq_size)
        attn_all = jnp.transpose(attn_parts, (1, 0, 2)).reshape(seq_len, -1)
        velocity = jnp.dot(attn_all, out_rows, preferred_element_type=jnp.float32)
        noise_level = SDE_NOISE * SDE_NOISE * time_now / (1.0 - time_now)
        std_dev = jnp.sqrt(noise_level * step_size)
        drift = velocity + noise_level / (2.0 * time_now) * (state + (1.0 - time_now) * velocity)
        mean_next = state - step_size * drift
        noise_now = step_noise[section, 0].astype(jnp.float32)
        state = mean_next + std_dev * noise_now
        factor = (
            my_coef[section]
            * -step_size
            * (1.0 + noise_level * (1.0 - time_now) / (2.0 * time_now))
            / std_dev
        )
        score_list.append((factor * noise_now).astype(jnp.bfloat16))
        attn_list.append(attn_all)
    attn_both = jnp.stack(attn_list, 0)
    score_both = jnp.stack(score_list, 0)
    rows = attn_both.shape[2]
    attn_halves = attn_both.reshape(attn_both.shape[0], attn_both.shape[1], 2, rows // 2)
    part = lax.dot_general(
        attn_halves, score_both, (((0, 1), (0, 1)), ((), ())), preferred_element_type=jnp.float32
    )
    part = reduce_pair(part, "grp")
    part = part.reshape(2, rows // 4, -1)
    part = reduce_pair(part, "xh")
    part = part.reshape(z_size, rows // (4 * z_size), -1)
    part = lax.all_to_all(part.astype(jnp.bfloat16), "z", 0, 0, tiled=True)
    out_grad = jnp.sum(part.astype(jnp.float32), 0)
    return (state[None], loss_value, out_grad)


def solution(mesh):
    grp, dp, seq = (mesh.shape[a] for a in ("grp", "dp", "seq"))
    xh, xl = 2, 2
    z_size, y_size = dp // xh, seq // xl
    fine = Mesh(
        mesh.devices.reshape(grp, xh, z_size, y_size, xl), ("grp", "xh", "z", "y", "xl")
    )
    samples = SAMPLE_AXES
    features = FEATURE_AXES

    def body(*args):
        return on_device(*args, z_size=z_size, seq_size=seq)

    return jax.shard_map(
        body,
        mesh=fine,
        in_specs=(
            P(samples, None, features),
            P(None, samples, None, features),
            P(),
            P(None, features, samples),
            P(samples, features),
            P(),
            P(),
            P(samples),
            P(),
        ),
        out_specs=(P(samples, None, features), P(), P(samples, features)),
        check_vma=False,
    )
```

```python
import jax
import jax.numpy as jnp
from jax import lax
from jax.sharding import Mesh
from jax.sharding import PartitionSpec as P

HD = 64
TSTEPS = 10
GSIZE = 8


SDE_NOISE = 0.7
CLIP_RANGE = 0.2
REWARD_FLOOR = 0.75
NORM_EPS = 1e-06

SAMPLE_AXES = ("grp", "xh", "z")
FEATURE_AXES = ("y", "xl")


def advantages(rewards, group_ids):
    same_group = (group_ids[:, None] == group_ids[None, :]).astype(jnp.float32)
    centre = jnp.sum(same_group * rewards[None, :], 1) / GSIZE
    spread = jnp.sum(same_group * (rewards[None, :] - centre[:, None]) ** 2, 1) / GSIZE
    return (rewards - centre) / jnp.maximum(jnp.sqrt(spread), REWARD_FLOOR)


def policy_terms(advantage, log_ratio):
    ratios = jnp.exp(log_ratio)
    plain = ratios * advantage[None, :]
    bounded = jnp.clip(ratios, 1.0 - CLIP_RANGE, 1.0 + CLIP_RANGE) * advantage[None, :]
    count = 2.0 * advantage.shape[0]
    loss_value = -jnp.sum(jnp.minimum(plain, bounded)) / count
    coef = jnp.where(plain <= bounded, -plain / count, jnp.float32(0.0))
    return (loss_value, coef)


def gather_all_to_all(x, axis_name, size):
    spread = jnp.broadcast_to(x[None], (size,) + x.shape)
    return lax.all_to_all(spread, axis_name, 0, 0, tiled=True)


def gather_pair(x, axis_name):
    other = lax.ppermute(x, axis_name, [(0, 1), (1, 0)])
    first = lax.axis_index(axis_name) == 0
    return jnp.where(first, jnp.stack([x, other]), jnp.stack([other, x]))


def reduce_pair(x, axis_name):
    me = lax.axis_index(axis_name)
    keep = lax.dynamic_index_in_dim(x, me, 0, keepdims=False)
    send = lax.dynamic_index_in_dim(x, 1 - me, 0, keepdims=False)
    sent = lax.ppermute(send.astype(jnp.bfloat16), axis_name, [(0, 1), (1, 0)])
    return keep + sent.astype(keep.dtype)


def on_device(
    latents,
    step_noise,
    ada_table,
    qkv_weight,
    out_weight,
    rewards,
    group_ids,
    time_index,
    log_ratio,
    z_size,
    seq_size,
):
    units = qkv_weight.shape[0] * qkv_weight.shape[1]
    qkv_t = jnp.transpose(qkv_weight, (2, 0, 1)).reshape(qkv_weight.shape[2], units)
    qkv_t = lax.all_gather(qkv_t, "z", axis=0, tiled=True)
    first_blocks = gather_all_to_all(latents[0].astype(jnp.bfloat16), FEATURE_AXES, seq_size)
    first_blocks, out_weight, qkv_t = lax.optimization_barrier((first_blocks, out_weight, qkv_t))
    out_z = gather_all_to_all(out_weight, "z", z_size)
    swap = [(0, 1), (1, 0)]
    me_g, me_x = lax.axis_index("grp"), lax.axis_index("xh")
    from_x = lax.ppermute(qkv_t, "xh", swap)
    from_g = lax.ppermute(qkv_t, "grp", swap)
    from_gx = lax.ppermute(from_x, "grp", swap)
    block_rows = qkv_t.shape[0]
    weight_blocks = [
        ((me_g * 2 + me_x) * block_rows, qkv_t),
        ((me_g * 2 + 1 - me_x) * block_rows, from_x),
        (((1 - me_g) * 2 + me_x) * block_rows, from_g),
        (((1 - me_g) * 2 + 1 - me_x) * block_rows, from_gx),
    ]

    group_width = qkv_weight.shape[1]
    heads_here = group_width // HD
    samples = rewards.shape[0]
    seq_len = latents.shape[1]
    query_count = min(512, seq_len)
    advantage = advantages(rewards, group_ids)
    loss_value, coef = policy_terms(advantage, log_ratio)
    my_index = lax.axis_index(SAMPLE_AXES)
    chooser = (jnp.arange(samples, dtype=jnp.int32) == my_index).astype(jnp.float32)
    my_coef = jnp.sum(coef * chooser[None, :], 1)
    step_size = 1.0 / TSTEPS
    state = latents[0]
    attn_list = []
    score_list = []
    plan = jnp.arange(TSTEPS, dtype=jnp.int32)
    for section in range(2):
        index_now = time_index[0] + section
        time_now = 1.0 - index_now.astype(jnp.float32) / TSTEPS
        picker = (plan == index_now).astype(jnp.float32)
        modulate = jnp.sum(picker[:, None, None] * ada_table, 0)
        if section == 0:
            blocks = first_blocks
        else:
            blocks = gather_all_to_all(state.astype(jnp.bfloat16), FEATURE_AXES, seq_size)
        whole = jnp.transpose(blocks, (1, 0, 2)).reshape(seq_len, -1).astype(jnp.float32)
        centre = jnp.mean(whole, -1, keepdims=True)
        spread = jnp.mean((whole - centre) ** 2, -1, keepdims=True)
        normed = (
            (whole - centre) * lax.rsqrt(spread + NORM_EPS) * (1.0 + modulate[0][None, :])
            + modulate[1][None, :]
        ).astype(jnp.bfloat16)
        proj_sum = None
        for offset, block in weight_blocks:
            columns = lax.dynamic_slice_in_dim(normed, offset, block.shape[0], axis=1)
            term = jnp.dot(columns, block, preferred_element_type=jnp.float32)
            proj_sum = term if proj_sum is None else proj_sum + term
        proj_rows = proj_sum.astype(jnp.bfloat16)
        proj_rows = proj_rows.reshape(seq_len, 3, heads_here, HD)
        key_rows = proj_rows[:, 1]
        value_rows = proj_rows[:, 2]
        query_rows = proj_rows[0:query_count, 0]
        logits = jnp.einsum(
            "qhe,khe->hqk", query_rows, key_rows, preferred_element_type=jnp.float32
        ) * HD ** (-0.5)
        logits = logits - jnp.max(logits, -1, keepdims=True)
        weights = jnp.exp(logits)
        probs = (weights / jnp.sum(weights, -1, keepdims=True)).astype(jnp.bfloat16)
        attn_blocks = jnp.einsum(
            "hqk,khe->qhe", probs, value_rows, preferred_element_type=jnp.float32
        ).astype(jnp.bfloat16)
        attn = attn_blocks.reshape(seq_len, group_width)
        if section == 0:
            out_z, attn = lax.optimization_barrier((out_z, attn))
            out_rows = out_z.reshape(-1, out_weight.shape[1])
            out_rows = gather_pair(out_rows, "xh").reshape(-1, out_weight.shape[1])
            out_rows = gather_pair(out_rows, "grp").reshape(-1, out_weight.shape[1])
        attn_parts = gather_all_to_all(attn, FEATURE_AXES, seq_size)
        attn_all = jnp.transpose(attn_parts, (1, 0, 2)).reshape(seq_len, -1)
        velocity = jnp.dot(attn_all, out_rows, preferred_element_type=jnp.float32)
        noise_level = SDE_NOISE * SDE_NOISE * time_now / (1.0 - time_now)
        std_dev = jnp.sqrt(noise_level * step_size)
        drift = velocity + noise_level / (2.0 * time_now) * (state + (1.0 - time_now) * velocity)
        mean_next = state - step_size * drift
        noise_now = step_noise[section, 0].astype(jnp.float32)
        state = mean_next + std_dev * noise_now
        factor = (
            my_coef[section]
            * -step_size
            * (1.0 + noise_level * (1.0 - time_now) / (2.0 * time_now))
            / std_dev
        )
        score_list.append((factor * noise_now).astype(jnp.bfloat16))
        attn_list.append(attn_all)
    attn_both = jnp.stack(attn_list, 0)
    score_both = jnp.stack(score_list, 0)
    rows = attn_both.shape[2]
    attn_halves = attn_both.reshape(attn_both.shape[0], attn_both.shape[1], 2, rows // 2)
    part = lax.dot_general(
        attn_halves, score_both, (((0, 1), (0, 1)), ((), ())), preferred_element_type=jnp.float32
    )
    part = reduce_pair(part, "grp")
    part = part.reshape(2, rows // 4, -1)
    part = reduce_pair(part, "xh")
    part = part.reshape(z_size, rows // (4 * z_size), -1)
    part = lax.all_to_all(part.astype(jnp.bfloat16), "z", 0, 0, tiled=True)
    out_grad = jnp.sum(part.astype(jnp.float32), 0)
    return (state[None], loss_value, out_grad)


def solution(mesh):
    grp, dp, seq = (mesh.shape[a] for a in ("grp", "dp", "seq"))
    xh, xl = 2, 2
    z_size, y_size = dp // xh, seq // xl
    fine = Mesh(
        mesh.devices.reshape(grp, xh, z_size, y_size, xl), ("grp", "xh", "z", "y", "xl")
    )
    samples = SAMPLE_AXES
    features = FEATURE_AXES

    def body(*args):
        return on_device(*args, z_size=z_size, seq_size=seq)

    return jax.shard_map(
        body,
        mesh=fine,
        in_specs=(
            P(samples, None, features),
            P(None, samples, None, features),
            P(),
            P(None, features, samples),
            P(samples, features),
            P(),
            P(),
            P(samples),
            P(),
        ),
        out_specs=(P(samples, None, features), P(), P(samples, features)),
        check_vma=False,
    )
```
